128 devices in a mesh: seq: 16 (over x, y), head: 8 (over z, core).
Axes of the slice: x: 4, y: 4, z: 4, core: 2. Of those that a mesh axis runs over, the one named last changes fastest.
Arguments:
- ssd_input: bfloat16 [4096, 8192], P('seq', 'head'), may hold values from -6 to 6
- gate_input: bfloat16 [4096, 8192], P('seq', 'head'), may hold values from -6 to 6
- write_vectors: bfloat16 [4096, 2048], P('seq', 'head'), may hold values from -1 to 1
- read_vectors: bfloat16 [4096, 2048], P('seq', 'head'), may hold values from -6 to 6
- log_decay: float32 [4096, 128], P('seq', 'head'), may hold values from -1 to 0
- skip_gain: float32 [128], P('head'), may hold values from 0.5 to 1.5
- norm_gain: float32 [8192], P('head'), may hold values from 0.5 to 1.5
- out_weight: bfloat16 [8192, 8192], P(None, 'head'), may hold values from -0.0625 to 0.0625
- out_grad: bfloat16 [4096, 8192], P('seq', 'head'), may hold values from -6 to 6
Outputs:
- layer_out: bfloat16 [4096, 8192], P('seq', 'head')
- input_grad: bfloat16 [4096, 8192], P('seq', 'head')
- gate_grad: bfloat16 [4096, 8192], P('seq', 'head')
- write_grad: bfloat16 [4096, 2048], P('seq', 'head')
- read_grad: bfloat16 [4096, 2048], P('seq', 'head')
- decay_grad: float32 [4096, 128], P('seq', 'head')
- weight_grad: bfloat16 [8192, 8192], P('seq', 'head')
The draws below stay inside these ranges and needn't reach their ends.
All inputs are finite; a program needn't handle non-finite values.
Results may differ from the reference program's by a relative error of at most 0.018.
Values may be sent and summed in bfloat16 or wider, within the bound.
No kernel may reach another device: no remote copies, remote signals or barrier semaphores. Data moves between devices by JAX's collectives and lax.ppermute only.
A program may use at most 192 MiB of HBM per device.

```python
import jax
import jax.numpy as jnp
from jax import lax

D = 8192
HALF_HEADS = 128
P_SIZE = 64
N = 256
G = 8
SPAN = 256
TOK_DEV = 256
SEQUENCE_TOKENS = 4096
N_SEQ = 16
N_HEAD = 8


def draw_log_decay(key, part):
    parallel_flows = jax.random.split(jax.random.fold_in(key, 17), 7)
    fast_share = 0.5
    fast_heads = jax.random.uniform(parallel_flows[0], (HALF_HEADS,)) < fast_share
    fast_rate = jax.random.uniform(parallel_flows[1], (HALF_HEADS,), minval=0.046, maxval=0.077)
    slow_rate = jax.random.uniform(parallel_flows[2], (HALF_HEADS,), minval=0.1, maxval=0.4) * (2.3026 / SEQUENCE_TOKENS)
    per_head_rate = jnp.where(fast_heads, fast_rate, slow_rate)
    jaggedness = jax.random.uniform(parallel_flows[3], (SEQUENCE_TOKENS, HALF_HEADS), minval=0.6, maxval=1.4)
    slab_scale_factor = jnp.exp(jax.random.uniform(parallel_flows[4], (SEQUENCE_TOKENS // TOK_DEV, HALF_HEADS), minval=-0.4, maxval=0.4))
    slab_scale_factor = jnp.repeat(slab_scale_factor, TOK_DEV, axis=0)
    spike_locations = jax.random.randint(parallel_flows[5], (3,), 0, SEQUENCE_TOKENS)
    spike_hit = jnp.any(jnp.arange(SEQUENCE_TOKENS)[:, None] == spike_locations[None, :], axis=1)
    spike_loss = jnp.log(jax.random.uniform(parallel_flows[6], (SEQUENCE_TOKENS, HALF_HEADS), minval=0.5, maxval=0.8))
    return (-per_head_rate[None, :] * jaggedness * slab_scale_factor + jnp.where(spike_hit[:, None], spike_loss, 0.0)).astype(jnp.float32)


def raised(drawn, own_key, source, target, shards_of, factor):
    owner, partner = [(jnp.arange(drawn.shape[axis_at]) // (drawn.shape[axis_at] // shards_of)).reshape([-1 if axis == axis_at else 1 for axis in range(drawn.ndim)]) for axis_at in (source, target)]
    chosen = jax.random.permutation(own_key, shards_of)[partner]
    strong = (owner == chosen) | (owner == (partner + shards_of // 2) % shards_of)
    return jnp.where(strong, factor * drawn, drawn)


def levels(own_key, shape, cuts, low, largest):
    loudness = 1.0
    for dim, blocks in cuts:
        draws = jax.random.uniform(jax.random.fold_in(jax.random.fold_in(own_key, 6), dim), (blocks,), jnp.float32, low / len(cuts), largest / len(cuts))
        loudness = loudness * jnp.repeat(jnp.exp(draws), shape[dim] // blocks).reshape((-1,) + (1,) * (len(shape) - 1 - dim))
    return loudness


def scatter_about(rng, shape, width, reach, cuts=(), kind=jnp.bfloat16):
    drawn = width * jax.random.normal(rng, shape, jnp.float32)
    if cuts:
        drawn = drawn * levels(rng, shape, cuts, -0.22, 0.18)
    return jnp.clip(drawn, -reach, reach).astype(kind)


def heavy_noise(own_key, dims, deviation, most, cuts, heavy, kind=jnp.bfloat16):
    result = deviation * jax.random.normal(own_key, dims, jnp.float32)
    if cuts:
        result = result * levels(own_key, dims, cuts, -0.22, 0.18)
    return jnp.clip(raised(result, jax.random.fold_in(own_key, 3), *heavy), -most, most).astype(kind)


def setup_inputs(seed: int = 0) -> dict:
    splits = jax.random.split(jax.random.key(seed), 10)
    return {
        "ssd_input": scatter_about(splits[0], (SEQUENCE_TOKENS, HALF_HEADS * P_SIZE), 1.0, 6.0, ((0, 16), (1, 8))),
        "gate_input": scatter_about(splits[1], (SEQUENCE_TOKENS, HALF_HEADS * P_SIZE), 1.0, 6.0, ((0, 16), (1, 8))),
        "write_vectors": scatter_about(splits[2], (SEQUENCE_TOKENS, G * N), (N ** -0.5), 1.0, ((0, 16), (1, 8))),
        "read_vectors": scatter_about(splits[3], (SEQUENCE_TOKENS, G * N), 1.0, 6.0, ((0, 16), (1, 8))),
        "log_decay": draw_log_decay(jax.random.fold_in(splits[9], 71), 0),
        "skip_gain": jnp.clip(0.5 + 1.0 * jax.random.uniform(splits[5], (HALF_HEADS,), jnp.float32) ** levels(splits[5], (HALF_HEADS,), ((0, 8),), -0.2, 0.2), 0.5, 1.5),
        "norm_gain": jnp.clip(0.5 + 1.0 * jax.random.uniform(splits[6], (HALF_HEADS * P_SIZE,), jnp.float32) ** levels(splits[6], (HALF_HEADS * P_SIZE,), ((0, 8),), -0.2, 0.2), 0.5, 1.5),
        "out_weight": scatter_about(splits[7], (D, HALF_HEADS * P_SIZE), (HALF_HEADS * P_SIZE) ** -0.5, 0.0625, ((1, 8),)),
        "out_grad": heavy_noise(splits[8], (SEQUENCE_TOKENS, D), 1.0, 6.0, ((0, 16), (1, 8)), (0, 1, 16, 2.0)),
    }


epsilon = 1e-05
highest = lax.Precision.HIGHEST

def block_scan(state_now, pieces):
    input_block, write_block, read_block, decay_block = pieces
    row_count = decay_block.shape[0]
    group_count, per_group = (state_now.shape[0], state_now.shape[1])
    input_heads = input_block.reshape(row_count, group_count, per_group, P_SIZE)
    write_heads = write_block.reshape(row_count, group_count, N)
    read_heads = read_block.reshape(row_count, group_count, N)
    cumulative = jnp.cumsum(decay_block, axis=0).reshape(row_count, group_count, per_group)
    by_head = jnp.transpose(cumulative, (1, 2, 0))
    causal = lax.broadcasted_iota(jnp.int32, (row_count, row_count), 0) >= lax.broadcasted_iota(jnp.int32, (row_count, row_count), 1)
    gap_table = jnp.where(causal, by_head[..., :, None] - by_head[..., None, :], 0.0)
    decay_table = jnp.where(causal, jnp.exp(gap_table), 0.0)
    scores = jnp.einsum('tgn,sgn->gts', read_heads, write_heads, precision=highest)
    weights = scores[:, None] * decay_table
    inner_sum = jnp.einsum('gkts,sgkp->tgkp', weights, input_heads, precision=highest)
    carried = jnp.einsum('tgn,gkpn->tgkp', read_heads, state_now, precision=highest)
    output = inner_sum + jnp.exp(cumulative)[..., None] * carried
    final_log = cumulative[-1]
    weighted = input_heads * jnp.exp(final_log[None] - cumulative)[..., None]
    fresh_state = jnp.einsum('sgkp,sgn->gkpn', weighted, write_heads, precision=highest)
    next_state = jnp.exp(final_log)[..., None, None] * state_now + fresh_state
    return (next_state, output.reshape(row_count, group_count * per_group * P_SIZE))

def ssd_run(inputs, writes, reading, decays, start_state):
    row_count = decays.shape[0]
    block_count = row_count // SPAN

    def in_blocks(operand):
        return operand.reshape(block_count, SPAN, operand.shape[1])
    final_state, outputs = lax.scan(block_scan, start_state, (in_blocks(inputs), in_blocks(writes), in_blocks(reading), in_blocks(decays)))
    return (outputs.reshape(row_count, outputs.shape[2]), final_state)

def gate_norm(ssd_out, inputs, gate_values, skip_gain, norm_gain):
    row_count = ssd_out.shape[0]
    head_count = skip_gain.shape[0]
    direct = (inputs.reshape(row_count, head_count, P_SIZE) * skip_gain[:, None]).reshape(row_count, head_count * P_SIZE)
    gated_vals = (ssd_out + direct) * jax.nn.silu(gate_values)
    grouped = gated_vals.reshape(row_count, -1, HALF_HEADS * P_SIZE // G)
    factor = lax.rsqrt(lax.optimization_barrier(jnp.mean(grouped * grouped, axis=2, keepdims=True)) + epsilon)
    return (grouped * factor).reshape(row_count, head_count * P_SIZE) * norm_gain

def reference(ssd_input, gate_input, write_vectors, read_vectors, log_decay, skip_gain, norm_gain, out_weight, out_grad):
    start_state = jnp.zeros((G, HALF_HEADS // G, P_SIZE, N), jnp.float32)

    def forward(inputs, gate_values, writes, reading, decays):
        ssd_out, final_state = ssd_run(inputs, writes, reading, decays, start_state)
        return gate_norm(ssd_out, inputs, gate_values, skip_gain, norm_gain)
    normed, pull_back = jax.vjp(forward, ssd_input.astype(jnp.float32), gate_input.astype(jnp.float32), write_vectors.astype(jnp.float32), read_vectors.astype(jnp.float32), log_decay)
    normed_half = normed.astype(jnp.bfloat16)
    head_width = HALF_HEADS * P_SIZE // N_HEAD
    layer_out = jnp.zeros((SEQUENCE_TOKENS, D), jnp.float32)
    for source in range(N_HEAD):
        partial_out = jnp.dot(normed_half[:, source * head_width:(source + 1) * head_width], out_weight[:, source * head_width:(source + 1) * head_width].T, preferred_element_type=jnp.float32)
        layer_out = layer_out + lax.optimization_barrier(partial_out.astype(jnp.bfloat16)).astype(jnp.float32)
    normed_grad = jnp.dot(out_grad, out_weight, preferred_element_type=jnp.float32)
    input_grad, gate_grad, write_grad, read_grad, decay_grad = pull_back(normed_grad)
    weight_grad = jnp.zeros((D, HALF_HEADS * P_SIZE), jnp.float32)
    for source in range(N_SEQ):
        partial_grad = jnp.dot(out_grad[source * TOK_DEV:(source + 1) * TOK_DEV].T, normed_half[source * TOK_DEV:(source + 1) * TOK_DEV], preferred_element_type=jnp.float32)
        weight_grad = weight_grad + lax.optimization_barrier(partial_grad.astype(jnp.bfloat16)).astype(jnp.float32)
    return (layer_out.astype(jnp.bfloat16), input_grad.astype(jnp.bfloat16), gate_grad.astype(jnp.bfloat16), write_grad.astype(jnp.bfloat16), read_grad.astype(jnp.bfloat16), decay_grad, weight_grad.astype(jnp.bfloat16))
```

```python
from functools import partial

import jax
import jax.numpy as jnp
from jax import lax
from jax.sharding import PartitionSpec as P

HALF_HEADS = 128
P_SIZE = 64
N = 256
G = 8
SPAN = 256


epsilon = 1e-05
highest = lax.Precision.HIGHEST


def log_scan(x, axis, reverse):
    count = lax.axis_size(axis)
    place = lax.axis_index(axis)
    decay, state = x
    incl = (decay, state)
    excl = (jnp.ones_like(decay), jnp.zeros_like(state))
    hop = 1
    while hop < count:
        if reverse:
            pairs = [(i + hop, i) for i in range(count - hop)]
            valid = place + hop < count
        else:
            pairs = [(i, i + hop) for i in range(count - hop)]
            valid = place >= hop
        got_decay = lax.ppermute(incl[0], axis, pairs)
        got_state = lax.ppermute(incl[1].astype(jnp.bfloat16), axis, pairs).astype(jnp.float32)
        got_decay = jnp.where(valid, got_decay, 1.0)
        got_state = jnp.where(valid, got_state, 0.0)
        excl = (got_decay * excl[0], excl[0][..., None, None] * got_state + excl[1])
        if hop * 2 < count:
            incl = (got_decay * incl[0], incl[0][..., None, None] * got_state + incl[1])
        hop *= 2
    return excl


def block_scan(state_now, pieces):
    input_block, write_block, read_block, decay_block = pieces
    row_count = decay_block.shape[0]
    group_count, per_group = (state_now.shape[0], state_now.shape[1])
    input_heads = input_block.reshape(row_count, group_count, per_group, P_SIZE)
    write_heads = write_block.reshape(row_count, group_count, N)
    read_heads = read_block.reshape(row_count, group_count, N)
    cumulative = jnp.cumsum(decay_block, axis=0).reshape(row_count, group_count, per_group)
    by_head = jnp.transpose(cumulative, (1, 2, 0))
    causal = lax.broadcasted_iota(jnp.int32, (row_count, row_count), 0) >= lax.broadcasted_iota(
        jnp.int32, (row_count, row_count), 1
    )
    gap_table = jnp.where(causal, by_head[..., :, None] - by_head[..., None, :], 0.0)
    decay_table = jnp.where(causal, jnp.exp(gap_table), 0.0)
    scores = jnp.einsum("tgn,sgn->gts", read_heads, write_heads, precision=highest)
    weights = scores[:, None] * decay_table
    inner_sum = jnp.einsum("gkts,sgkp->tgkp", weights, input_heads, precision=highest)
    carried = jnp.einsum("tgn,gkpn->tgkp", read_heads, state_now, precision=highest)
    output = inner_sum + jnp.exp(cumulative)[..., None] * carried
    final_log = cumulative[-1]
    weighted = input_heads * jnp.exp(final_log[None] - cumulative)[..., None]
    fresh_state = jnp.einsum("sgkp,sgn->gkpn", weighted, write_heads, precision=highest)
    next_state = jnp.exp(final_log)[..., None, None] * state_now + fresh_state
    return (next_state, output.reshape(row_count, group_count * per_group * P_SIZE))


def block_end(state_now, pieces):
    input_block, write_block, decay_block = pieces
    row_count = decay_block.shape[0]
    group_count, per_group = (state_now.shape[0], state_now.shape[1])
    input_heads = input_block.reshape(row_count, group_count, per_group, P_SIZE)
    write_heads = write_block.reshape(row_count, group_count, N)
    cumulative = jnp.cumsum(decay_block, axis=0).reshape(row_count, group_count, per_group)
    final_log = cumulative[-1]
    weighted = input_heads * jnp.exp(final_log[None] - cumulative)[..., None]
    fresh_state = jnp.einsum("sgkp,sgn->gkpn", weighted, write_heads, precision=highest)
    return (jnp.exp(final_log)[..., None, None] * state_now + fresh_state, None)


def in_blocks(operand):
    return operand.reshape(operand.shape[0] // SPAN, SPAN, operand.shape[1])


def ssd_run(inputs, writes, reading, decays, start_state):
    row_count = decays.shape[0]
    final_state, outputs = lax.scan(
        block_scan,
        start_state,
        (in_blocks(inputs), in_blocks(writes), in_blocks(reading), in_blocks(decays)),
    )
    return (outputs.reshape(row_count, outputs.shape[2]), final_state)


def gate_norm(ssd_out, inputs, gate_values, skip_gain, norm_gain):
    row_count = ssd_out.shape[0]
    head_count = skip_gain.shape[0]
    direct = (inputs.reshape(row_count, head_count, P_SIZE) * skip_gain[:, None]).reshape(
        row_count, head_count * P_SIZE
    )
    gated_vals = (ssd_out + direct) * jax.nn.silu(gate_values)
    grouped = gated_vals.reshape(row_count, -1, HALF_HEADS * P_SIZE // G)
    factor = lax.rsqrt(jnp.mean(grouped * grouped, axis=2, keepdims=True) + epsilon)
    return (grouped * factor).reshape(row_count, head_count * P_SIZE) * norm_gain


def combine(earlier, later):
    return (earlier[0] * later[0], later[0][..., None, None] * earlier[1] + later[1])


def per_device(
    ssd_input,
    gate_input,
    write_vectors,
    read_vectors,
    log_decay,
    skip_gain,
    norm_gain,
    out_weight,
    out_grad,
):
    row_count, head_count = log_decay.shape
    group_count = write_vectors.shape[1] // N
    per_group = head_count // group_count
    inputs = ssd_input.astype(jnp.float32)
    gate_values = gate_input.astype(jnp.float32)
    writes = write_vectors.astype(jnp.float32)
    reading = read_vectors.astype(jnp.float32)
    zero_state = jnp.zeros((group_count, per_group, P_SIZE, N), jnp.float32)
    own_state, unused = lax.scan(
        block_end, zero_state, (in_blocks(inputs), in_blocks(writes), in_blocks(log_decay))
    )
    cumulative = jnp.cumsum(log_decay, axis=0)
    own_decay = jnp.exp(cumulative[-1]).reshape(group_count, per_group)
    decay_before, start_state = log_scan((own_decay, own_state), "seq", False)
    (ssd_out, end_state), ssd_pull = jax.vjp(
        ssd_run, inputs, writes, reading, log_decay, start_state
    )
    norm_fn = partial(gate_norm, skip_gain=skip_gain, norm_gain=norm_gain)
    normed, norm_pull = jax.vjp(norm_fn, ssd_out, inputs, gate_values)
    normed_half = normed.astype(jnp.bfloat16)
    partial_out = jnp.einsum(
        "th,dh->td", normed_half, out_weight, preferred_element_type=jnp.float32
    )
    layer_out = lax.psum_scatter(
        partial_out.astype(jnp.bfloat16), "head", scatter_dimension=1, tiled=True
    )
    full_grad = lax.all_gather(out_grad, "head", axis=1, tiled=True)
    normed_grad = jnp.dot(full_grad, out_weight, preferred_element_type=jnp.float32)
    ssd_grad, skip_input_grad, gate_grad = norm_pull(normed_grad)
    scaled_grad = ssd_grad.reshape(row_count, group_count, per_group, P_SIZE) * jnp.exp(
        cumulative
    ).reshape(row_count, group_count, per_group, 1)
    state_direct = jnp.einsum(
        "tgkp,tgn->gkpn", scaled_grad, reading.reshape(row_count, group_count, N), precision=highest
    )
    decay_after, end_grad = log_scan((own_decay, state_direct), "seq", True)
    input_part, write_grad, read_grad, decay_grad, start_grad = ssd_pull((ssd_grad, end_grad))
    input_grad = skip_input_grad + input_part
    weight_grad = lax.psum_scatter(
        jnp.einsum("td,th->dh", full_grad, normed_half, preferred_element_type=jnp.float32).astype(
            jnp.bfloat16
        ),
        "seq",
        scatter_dimension=0,
        tiled=True,
    )
    return (
        layer_out,
        input_grad.astype(jnp.bfloat16),
        gate_grad.astype(jnp.bfloat16),
        write_grad.astype(jnp.bfloat16),
        read_grad.astype(jnp.bfloat16),
        decay_grad,
        weight_grad,
    )


def solution(mesh):
    in_specs = (
        P("seq", "head"),
        P("seq", "head"),
        P("seq", "head"),
        P("seq", "head"),
        P("seq", "head"),
        P("head"),
        P("head"),
        P(None, "head"),
        P("seq", "head"),
    )
    out_specs = (
        P("seq", "head"),
        P("seq", "head"),
        P("seq", "head"),
        P("seq", "head"),
        P("seq", "head"),
        P("seq", "head"),
        P("seq", "head"),
    )
    return jax.shard_map(
        per_device, mesh=mesh, in_specs=in_specs, out_specs=out_specs, check_vma=False
    )
```

```python
from functools import partial

import jax
import jax.numpy as jnp
from jax import lax
from jax.sharding import PartitionSpec as P

HALF_HEADS = 128
P_SIZE = 64
N = 256
G = 8
SPAN = 256


epsilon = 1e-05
highest = lax.Precision.HIGHEST


def log_scan(x, axis, reverse):
    count = lax.axis_size(axis)
    place = lax.axis_index(axis)
    decay, state = x
    incl = (decay, state)
    excl = (jnp.ones_like(decay), jnp.zeros_like(state))
    hop = 1
    while hop < count:
        if reverse:
            pairs = [(i + hop, i) for i in range(count - hop)]
            valid = place + hop < count
        else:
            pairs = [(i, i + hop) for i in range(count - hop)]
            valid = place >= hop
        got_decay = lax.ppermute(incl[0], axis, pairs)
        got_state = lax.ppermute(incl[1].astype(jnp.bfloat16), axis, pairs).astype(jnp.float32)
        got_decay = jnp.where(valid, got_decay, 1.0)
        got_state = jnp.where(valid, got_state, 0.0)
        excl = (got_decay * excl[0], excl[0][..., None, None] * got_state + excl[1])
        if hop * 2 < count:
            incl = (got_decay * incl[0], incl[0][..., None, None] * got_state + incl[1])
        hop *= 2
    return excl


def block_scan(state_now, pieces):
    input_block, write_block, read_block, decay_block = pieces
    row_count = decay_block.shape[0]
    group_count, per_group = (state_now.shape[0], state_now.shape[1])
    input_heads = input_block.reshape(row_count, group_count, per_group, P_SIZE)
    write_heads = write_block.reshape(row_count, group_count, N)
    read_heads = read_block.reshape(row_count, group_count, N)
    cumulative = jnp.cumsum(decay_block, axis=0).reshape(row_count, group_count, per_group)
    by_head = jnp.transpose(cumulative, (1, 2, 0))
    causal = lax.broadcasted_iota(jnp.int32, (row_count, row_count), 0) >= lax.broadcasted_iota(
        jnp.int32, (row_count, row_count), 1
    )
    gap_table = jnp.where(causal, by_head[..., :, None] - by_head[..., None, :], 0.0)
    decay_table = jnp.where(causal, jnp.exp(gap_table), 0.0)
    scores = jnp.einsum("tgn,sgn->gts", read_heads, write_heads, precision=highest)
    weights = scores[:, None] * decay_table
    inner_sum = jnp.einsum("gkts,sgkp->tgkp", weights, input_heads, precision=highest)
    carried = jnp.einsum("tgn,gkpn->tgkp", read_heads, state_now, precision=highest)
    output = inner_sum + jnp.exp(cumulative)[..., None] * carried
    final_log = cumulative[-1]
    weighted = input_heads * jnp.exp(final_log[None] - cumulative)[..., None]
    fresh_state = jnp.einsum("sgkp,sgn->gkpn", weighted, write_heads, precision=highest)
    next_state = jnp.exp(final_log)[..., None, None] * state_now + fresh_state
    return (next_state, output.reshape(row_count, group_count * per_group * P_SIZE))


def block_end(state_now, pieces):
    input_block, write_block, decay_block = pieces
    row_count = decay_block.shape[0]
    group_count, per_group = (state_now.shape[0], state_now.shape[1])
    input_heads = input_block.reshape(row_count, group_count, per_group, P_SIZE)
    write_heads = write_block.reshape(row_count, group_count, N)
    cumulative = jnp.cumsum(decay_block, axis=0).reshape(row_count, group_count, per_group)
    final_log = cumulative[-1]
    weighted = input_heads * jnp.exp(final_log[None] - cumulative)[..., None]
    fresh_state = jnp.einsum("sgkp,sgn->gkpn", weighted, write_heads, precision=highest)
    return (jnp.exp(final_log)[..., None, None] * state_now + fresh_state, None)


def in_blocks(operand):
    return operand.reshape(operand.shape[0] // SPAN, SPAN, operand.shape[1])


def ssd_run(inputs, writes, reading, decays, start_state):
    row_count = decays.shape[0]
    final_state, outputs = lax.scan(
        block_scan,
        start_state,
        (in_blocks(inputs), in_blocks(writes), in_blocks(reading), in_blocks(decays)),
    )
    return (outputs.reshape(row_count, outputs.shape[2]), final_state)


def gate_norm(ssd_out, inputs, gate_values, skip_gain, norm_gain):
    row_count = ssd_out.shape[0]
    head_count = skip_gain.shape[0]
    direct = (inputs.reshape(row_count, head_count, P_SIZE) * skip_gain[:, None]).reshape(
        row_count, head_count * P_SIZE
    )
    gated_vals = (ssd_out + direct) * jax.nn.silu(gate_values)
    grouped = gated_vals.reshape(row_count, -1, HALF_HEADS * P_SIZE // G)
    factor = lax.rsqrt(jnp.mean(grouped * grouped, axis=2, keepdims=True) + epsilon)
    return (grouped * factor).reshape(row_count, head_count * P_SIZE) * norm_gain


def combine(earlier, later):
    return (earlier[0] * later[0], later[0][..., None, None] * earlier[1] + later[1])


def per_device(
    ssd_input,
    gate_input,
    write_vectors,
    read_vectors,
    log_decay,
    skip_gain,
    norm_gain,
    out_weight,
    out_grad,
):
    row_count, head_count = log_decay.shape
    group_count = write_vectors.shape[1] // N
    per_group = head_count // group_count
    inputs = ssd_input.astype(jnp.float32)
    gate_values = gate_input.astype(jnp.float32)
    writes = write_vectors.astype(jnp.float32)
    reading = read_vectors.astype(jnp.float32)
    zero_state = jnp.zeros((group_count, per_group, P_SIZE, N), jnp.float32)
    own_state, unused = lax.scan(
        block_end, zero_state, (in_blocks(inputs), in_blocks(writes), in_blocks(log_decay))
    )
    cumulative = jnp.cumsum(log_decay, axis=0)
    own_decay = jnp.exp(cumulative[-1]).reshape(group_count, per_group)
    decay_before, start_state = log_scan((own_decay, own_state), "seq", False)
    (ssd_out, end_state), ssd_pull = jax.vjp(
        ssd_run, inputs, writes, reading, log_decay, start_state
    )
    norm_fn = partial(gate_norm, skip_gain=skip_gain, norm_gain=norm_gain)
    normed, norm_pull = jax.vjp(norm_fn, ssd_out, inputs, gate_values)
    normed_half = normed.astype(jnp.bfloat16)
    partial_out = jnp.einsum(
        "th,dh->td", normed_half, out_weight, preferred_element_type=jnp.float32
    )
    layer_out = lax.psum_scatter(
        partial_out.astype(jnp.bfloat16), "head", scatter_dimension=1, tiled=True
    )
    full_grad = lax.all_gather(out_grad, "head", axis=1, tiled=True)
    normed_grad = jnp.dot(full_grad, out_weight, preferred_element_type=jnp.float32)
    ssd_grad, skip_input_grad, gate_grad = norm_pull(normed_grad)
    scaled_grad = ssd_grad.reshape(row_count, group_count, per_group, P_SIZE) * jnp.exp(
        cumulative
    ).reshape(row_count, group_count, per_group, 1)
    state_direct = jnp.einsum(
        "tgkp,tgn->gkpn", scaled_grad, reading.reshape(row_count, group_count, N), precision=highest
    )
    decay_after, end_grad = log_scan((own_decay, state_direct), "seq", True)
    input_part, write_grad, read_grad, decay_grad, start_grad = ssd_pull((ssd_grad, end_grad))
    input_grad = skip_input_grad + input_part
    seq_count = lax.axis_size("seq")
    feature_count = full_grad.shape[1]
    grad_columns = lax.all_to_all(
        full_grad.reshape(row_count, seq_count, feature_count // seq_count),
        "seq",
        split_axis=1,
        concat_axis=0,
        tiled=True,
    ).reshape(seq_count * row_count, feature_count // seq_count)
    all_normed = lax.all_gather(normed_half, "seq", axis=0, tiled=True)
    weight_grad = jnp.einsum(
        "td,th->dh", grad_columns, all_normed, preferred_element_type=jnp.float32
    ).astype(jnp.bfloat16)
    return (
        layer_out,
        input_grad.astype(jnp.bfloat16),
        gate_grad.astype(jnp.bfloat16),
        write_grad.astype(jnp.bfloat16),
        read_grad.astype(jnp.bfloat16),
        decay_grad,
        weight_grad,
    )


def solution(mesh):
    in_specs = (
        P("seq", "head"),
        P("seq", "head"),
        P("seq", "head"),
        P("seq", "head"),
        P("seq", "head"),
        P("head"),
        P("head"),
        P(None, "head"),
        P("seq", "head"),
    )
    out_specs = (
        P("seq", "head"),
        P("seq", "head"),
        P("seq", "head"),
        P("seq", "head"),
        P("seq", "head"),
        P("seq", "head"),
        P("seq", "head"),
    )
    return jax.shard_map(
        per_device, mesh=mesh, in_specs=in_specs, out_specs=out_specs, check_vma=False
    )
```

```python
from functools import partial

import jax
import jax.numpy as jnp
from jax import lax
from jax.sharding import Mesh, PartitionSpec as P

HALF_HEADS = 128
P_SIZE = 64
N = 256
G = 8
SPAN = 256
SEQ = ("sx", "sy")


epsilon = 1e-05
highest = lax.Precision.HIGHEST


def log_scan(x, axis, reverse):
    count = lax.axis_size(axis)
    place = lax.axis_index(axis)
    decay, state = x
    incl = (decay, state)
    excl = (jnp.ones_like(decay), jnp.zeros_like(state))
    hop = 1
    while hop < count:
        if reverse:
            pairs = [(i + hop, i) for i in range(count - hop)]
            valid = place + hop < count
        else:
            pairs = [(i, i + hop) for i in range(count - hop)]
            valid = place >= hop
        got_decay = lax.ppermute(incl[0], axis, pairs)
        got_state = lax.ppermute(incl[1].astype(jnp.bfloat16), axis, pairs).astype(jnp.float32)
        got_decay = jnp.where(valid, got_decay, 1.0)
        got_state = jnp.where(valid, got_state, 0.0)
        excl = (got_decay * excl[0], excl[0][..., None, None] * got_state + excl[1])
        if hop * 2 < count:
            incl = (got_decay * incl[0], incl[0][..., None, None] * got_state + incl[1])
        hop *= 2
    return excl


def block_scan(state_now, pieces):
    input_block, write_block, read_block, decay_block = pieces
    row_count = decay_block.shape[0]
    group_count, per_group = (state_now.shape[0], state_now.shape[1])
    input_heads = input_block.reshape(row_count, group_count, per_group, P_SIZE)
    write_heads = write_block.reshape(row_count, group_count, N)
    read_heads = read_block.reshape(row_count, group_count, N)
    cumulative = jnp.cumsum(decay_block, axis=0).reshape(row_count, group_count, per_group)
    by_head = jnp.transpose(cumulative, (1, 2, 0))
    causal = lax.broadcasted_iota(jnp.int32, (row_count, row_count), 0) >= lax.broadcasted_iota(
        jnp.int32, (row_count, row_count), 1
    )
    gap_table = jnp.where(causal, by_head[..., :, None] - by_head[..., None, :], 0.0)
    decay_table = jnp.where(causal, jnp.exp(gap_table), 0.0)
    scores = jnp.einsum("tgn,sgn->gts", read_heads, write_heads, precision=highest)
    weights = scores[:, None] * decay_table
    inner_sum = jnp.einsum("gkts,sgkp->tgkp", weights, input_heads, precision=highest)
    carried = jnp.einsum("tgn,gkpn->tgkp", read_heads, state_now, precision=highest)
    output = inner_sum + jnp.exp(cumulative)[..., None] * carried
    final_log = cumulative[-1]
    weighted = input_heads * jnp.exp(final_log[None] - cumulative)[..., None]
    fresh_state = jnp.einsum("sgkp,sgn->gkpn", weighted, write_heads, precision=highest)
    next_state = jnp.exp(final_log)[..., None, None] * state_now + fresh_state
    return (next_state, output.reshape(row_count, group_count * per_group * P_SIZE))


def block_end(state_now, pieces):
    input_block, write_block, decay_block = pieces
    row_count = decay_block.shape[0]
    group_count, per_group = (state_now.shape[0], state_now.shape[1])
    input_heads = input_block.reshape(row_count, group_count, per_group, P_SIZE)
    write_heads = write_block.reshape(row_count, group_count, N)
    cumulative = jnp.cumsum(decay_block, axis=0).reshape(row_count, group_count, per_group)
    final_log = cumulative[-1]
    weighted = input_heads * jnp.exp(final_log[None] - cumulative)[..., None]
    fresh_state = jnp.einsum("sgkp,sgn->gkpn", weighted, write_heads, precision=highest)
    return (jnp.exp(final_log)[..., None, None] * state_now + fresh_state, None)


def in_blocks(operand):
    return operand.reshape(operand.shape[0] // SPAN, SPAN, operand.shape[1])


def ssd_run(inputs, writes, reading, decays, start_state):
    row_count = decays.shape[0]
    final_state, outputs = lax.scan(
        block_scan,
        start_state,
        (in_blocks(inputs), in_blocks(writes), in_blocks(reading), in_blocks(decays)),
    )
    return (outputs.reshape(row_count, outputs.shape[2]), final_state)


def gate_norm(ssd_out, inputs, gate_values, skip_gain, norm_gain):
    row_count = ssd_out.shape[0]
    head_count = skip_gain.shape[0]
    direct = (inputs.reshape(row_count, head_count, P_SIZE) * skip_gain[:, None]).reshape(
        row_count, head_count * P_SIZE
    )
    gated_vals = (ssd_out + direct) * jax.nn.silu(gate_values)
    grouped = gated_vals.reshape(row_count, -1, HALF_HEADS * P_SIZE // G)
    factor = lax.rsqrt(jnp.mean(grouped * grouped, axis=2, keepdims=True) + epsilon)
    return (grouped * factor).reshape(row_count, head_count * P_SIZE) * norm_gain


def combine(earlier, later):
    return (earlier[0] * later[0], later[0][..., None, None] * earlier[1] + later[1])


def per_device(
    ssd_input,
    gate_input,
    write_vectors,
    read_vectors,
    log_decay,
    skip_gain,
    norm_gain,
    out_weight,
    out_grad,
):
    row_count, head_count = log_decay.shape
    group_count = write_vectors.shape[1] // N
    per_group = head_count // group_count
    inputs = ssd_input.astype(jnp.float32)
    gate_values = gate_input.astype(jnp.float32)
    writes = write_vectors.astype(jnp.float32)
    reading = read_vectors.astype(jnp.float32)
    zero_state = jnp.zeros((group_count, per_group, P_SIZE, N), jnp.float32)
    own_state, unused = lax.scan(
        block_end, zero_state, (in_blocks(inputs), in_blocks(writes), in_blocks(log_decay))
    )
    cumulative = jnp.cumsum(log_decay, axis=0)
    own_decay = jnp.exp(cumulative[-1]).reshape(group_count, per_group)
    decay_before, start_state = log_scan((own_decay, own_state), SEQ, False)
    (ssd_out, end_state), ssd_pull = jax.vjp(
        ssd_run, inputs, writes, reading, log_decay, start_state
    )
    norm_fn = partial(gate_norm, skip_gain=skip_gain, norm_gain=norm_gain)
    normed, norm_pull = jax.vjp(norm_fn, ssd_out, inputs, gate_values)
    normed_half = normed.astype(jnp.bfloat16)
    partial_out = jnp.einsum(
        "th,dh->td", normed_half, out_weight, preferred_element_type=jnp.float32
    )
    layer_out = lax.psum_scatter(
        partial_out.astype(jnp.bfloat16), "head", scatter_dimension=1, tiled=True
    )
    full_grad = lax.all_gather(out_grad, "head", axis=1, tiled=True)
    normed_grad = jnp.dot(full_grad, out_weight, preferred_element_type=jnp.float32)
    ssd_grad, skip_input_grad, gate_grad = norm_pull(normed_grad)
    scaled_grad = ssd_grad.reshape(row_count, group_count, per_group, P_SIZE) * jnp.exp(
        cumulative
    ).reshape(row_count, group_count, per_group, 1)
    state_direct = jnp.einsum(
        "tgkp,tgn->gkpn", scaled_grad, reading.reshape(row_count, group_count, N), precision=highest
    )
    decay_after, end_grad = log_scan((own_decay, state_direct), SEQ, True)
    input_part, write_grad, read_grad, decay_grad, start_grad = ssd_pull((ssd_grad, end_grad))
    input_grad = skip_input_grad + input_part
    rows = lax.axis_size("sx")
    cols = lax.axis_size("sy")
    feature_count = full_grad.shape[1]
    block = feature_count // (rows * cols)
    grad_columns = lax.all_to_all(
        full_grad.reshape(row_count, rows, cols, block),
        "sy",
        split_axis=2,
        concat_axis=0,
        tiled=True,
    ).reshape(cols * row_count, rows, block)
    row_normed = lax.all_gather(normed_half, "sy", axis=0, tiled=True)
    row_partial = jnp.einsum(
        "txd,th->xdh", grad_columns, row_normed, preferred_element_type=jnp.float32
    ).astype(jnp.bfloat16)
    weight_grad = lax.psum_scatter(row_partial, "sx", scatter_dimension=0, tiled=True).reshape(
        block, row_normed.shape[1]
    )
    return (
        layer_out,
        input_grad.astype(jnp.bfloat16),
        gate_grad.astype(jnp.bfloat16),
        write_grad.astype(jnp.bfloat16),
        read_grad.astype(jnp.bfloat16),
        decay_grad,
        weight_grad,
    )


def solution(mesh):
    in_specs = (
        P(SEQ, "head"),
        P(SEQ, "head"),
        P(SEQ, "head"),
        P(SEQ, "head"),
        P(SEQ, "head"),
        P("head"),
        P("head"),
        P(None, "head"),
        P(SEQ, "head"),
    )
    out_specs = (
        P(SEQ, "head"),
        P(SEQ, "head"),
        P(SEQ, "head"),
        P(SEQ, "head"),
        P(SEQ, "head"),
        P(SEQ, "head"),
        P(SEQ, "head"),
    )
    rows = mesh.devices.shape[0] // 4
    grid = Mesh(mesh.devices.reshape(rows, 4, mesh.devices.shape[1]), ("sx", "sy", "head"))
    return jax.shard_map(
        per_device, mesh=grid, in_specs=in_specs, out_specs=out_specs, check_vma=False
    )
```

```python
from functools import partial

import jax
import jax.numpy as jnp
from jax import lax
from jax.sharding import Mesh, PartitionSpec as P


HALF_HEADS = 128
P_SIZE = 64
N = 256
G = 8
SPAN = 256
SEQ = ("sx", "sy")


epsilon = 1e-05
highest = lax.Precision.HIGHEST


def log_scan(x, axis, reverse, before_send=None, after_receive=None):
    count = lax.axis_size(axis)
    place = lax.axis_index(axis)
    decay, state = x
    incl = (decay, state)
    excl = (jnp.ones_like(decay), jnp.zeros_like(state))
    hop = 1
    while hop < count:
        if reverse:
            pairs = [(i + hop, i) for i in range(count - hop)]
            valid = place + hop < count
        else:
            pairs = [(i, i + hop) for i in range(count - hop)]
            valid = place >= hop
        if before_send is not None:
            incl = (incl[0], before_send(hop, incl[1]))
        got_decay = lax.ppermute(incl[0], axis, pairs)
        got_state = lax.ppermute(incl[1].astype(jnp.bfloat16), axis, pairs).astype(jnp.float32)
        if after_receive is not None:
            got_state = after_receive(hop, got_state)
        got_decay = jnp.where(valid, got_decay, 1.0)
        got_state = jnp.where(valid, got_state, 0.0)
        excl = (got_decay * excl[0], excl[0][..., None, None] * got_state + excl[1])
        if hop * 2 < count:
            incl = (got_decay * incl[0], incl[0][..., None, None] * got_state + incl[1])
        hop *= 2
    return excl


def block_scan(state_now, pieces):
    input_block, write_block, read_block, decay_block = pieces
    row_count = decay_block.shape[0]
    group_count, per_group = (state_now.shape[0], state_now.shape[1])
    input_heads = input_block.reshape(row_count, group_count, per_group, P_SIZE)
    write_heads = write_block.reshape(row_count, group_count, N)
    read_heads = read_block.reshape(row_count, group_count, N)
    cumulative = jnp.cumsum(decay_block, axis=0).reshape(row_count, group_count, per_group)
    by_head = jnp.transpose(cumulative, (1, 2, 0))
    causal = lax.broadcasted_iota(jnp.int32, (row_count, row_count), 0) >= lax.broadcasted_iota(
        jnp.int32, (row_count, row_count), 1
    )
    gap_table = jnp.where(causal, by_head[..., :, None] - by_head[..., None, :], 0.0)
    decay_table = jnp.where(causal, jnp.exp(gap_table), 0.0)
    scores = jnp.einsum("tgn,sgn->gts", read_heads, write_heads, precision=highest)
    weights = scores[:, None] * decay_table
    inner_sum = jnp.einsum("gkts,sgkp->tgkp", weights, input_heads, precision=highest)
    carried = jnp.einsum("tgn,gkpn->tgkp", read_heads, state_now, precision=highest)
    output = inner_sum + jnp.exp(cumulative)[..., None] * carried
    final_log = cumulative[-1]
    weighted = input_heads * jnp.exp(final_log[None] - cumulative)[..., None]
    fresh_state = jnp.einsum("sgkp,sgn->gkpn", weighted, write_heads, precision=highest)
    next_state = jnp.exp(final_log)[..., None, None] * state_now + fresh_state
    return (next_state, output.reshape(row_count, group_count * per_group * P_SIZE))


def block_end(state_now, pieces):
    input_block, write_block, decay_block = pieces
    row_count = decay_block.shape[0]
    group_count, per_group = (state_now.shape[0], state_now.shape[1])
    input_heads = input_block.reshape(row_count, group_count, per_group, P_SIZE)
    write_heads = write_block.reshape(row_count, group_count, N)
    cumulative = jnp.cumsum(decay_block, axis=0).reshape(row_count, group_count, per_group)
    final_log = cumulative[-1]
    weighted = input_heads * jnp.exp(final_log[None] - cumulative)[..., None]
    fresh_state = jnp.einsum("sgkp,sgn->gkpn", weighted, write_heads, precision=highest)
    return (jnp.exp(final_log)[..., None, None] * state_now + fresh_state, None)


def in_blocks(operand):
    return operand.reshape(operand.shape[0] // SPAN, SPAN, operand.shape[1])


def ssd_run(inputs, writes, reading, decays, start_state):
    row_count = decays.shape[0]
    final_state, outputs = lax.scan(
        block_scan,
        start_state,
        (in_blocks(inputs), in_blocks(writes), in_blocks(reading), in_blocks(decays)),
    )
    return (outputs.reshape(row_count, outputs.shape[2]), final_state)


def gate_norm(ssd_out, inputs, gate_values, skip_gain, norm_gain):
    row_count = ssd_out.shape[0]
    head_count = skip_gain.shape[0]
    direct = (inputs.reshape(row_count, head_count, P_SIZE) * skip_gain[:, None]).reshape(
        row_count, head_count * P_SIZE
    )
    gated_vals = (ssd_out + direct) * jax.nn.silu(gate_values)
    grouped = gated_vals.reshape(row_count, -1, HALF_HEADS * P_SIZE // G)
    factor = lax.rsqrt(jnp.mean(grouped * grouped, axis=2, keepdims=True) + epsilon)
    return (grouped * factor).reshape(row_count, head_count * P_SIZE) * norm_gain


def per_device(
    ssd_input,
    gate_input,
    write_vectors,
    read_vectors,
    log_decay,
    skip_gain,
    norm_gain,
    out_weight,
    out_grad,
):
    row_count, head_count = log_decay.shape
    group_count = write_vectors.shape[1] // N
    per_group = head_count // group_count
    inputs = ssd_input.astype(jnp.float32)
    gate_values = gate_input.astype(jnp.float32)
    writes = write_vectors.astype(jnp.float32)
    reading = read_vectors.astype(jnp.float32)
    zero_state = jnp.zeros((group_count, per_group, P_SIZE, N), jnp.float32)
    own_state, _ = lax.scan(
        block_end, zero_state, (in_blocks(inputs), in_blocks(writes), in_blocks(log_decay))
    )
    cumulative = jnp.cumsum(log_decay, axis=0)
    own_decay = jnp.exp(cumulative[-1]).reshape(group_count, per_group)
    rows = lax.axis_size("sx")
    cols = lax.axis_size("sy")
    full_grad = lax.all_gather(out_grad, "head", axis=1, tiled=True)
    feature_count = full_grad.shape[1]
    block = feature_count // (rows * cols)
    tied = {}

    def during_forward(hop, state):
        if hop == 4:
            state, tied["grad"] = lax.optimization_barrier((state, full_grad))
        if hop == 8:
            columns = lax.all_to_all(
                tied["grad"].reshape(row_count, rows, cols, block),
                "sy",
                split_axis=2,
                concat_axis=0,
                tiled=True,
            ).reshape(cols * row_count, rows, block)
            normed_grad = jnp.dot(tied["grad"], out_weight, preferred_element_type=jnp.float32)
            state, tied["columns"], tied["normed_grad"] = lax.optimization_barrier(
                (state, columns, normed_grad)
            )
        return state

    def during_backward(hop, got_state):
        if hop == 2:
            got_state, tied["late_normed"] = lax.optimization_barrier((got_state, normed_half))
        return got_state

    _, start_state = log_scan((own_decay, own_state), SEQ, False, during_forward)
    (ssd_out, end_state), ssd_pull = jax.vjp(
        ssd_run, inputs, writes, reading, log_decay, start_state
    )
    norm_fn = partial(gate_norm, skip_gain=skip_gain, norm_gain=norm_gain)
    normed, norm_pull = jax.vjp(norm_fn, ssd_out, inputs, gate_values)
    normed_half = normed.astype(jnp.bfloat16)
    partial_out = jnp.einsum(
        "th,dh->td", normed_half, out_weight, preferred_element_type=jnp.float32
    )
    layer_out = lax.psum_scatter(
        partial_out.astype(jnp.bfloat16), "head", scatter_dimension=1, tiled=True
    )
    ssd_grad, skip_input_grad, gate_grad = norm_pull(tied["normed_grad"])
    scaled_grad = ssd_grad.reshape(row_count, group_count, per_group, P_SIZE) * jnp.exp(
        cumulative
    ).reshape(row_count, group_count, per_group, 1)
    state_direct = jnp.einsum(
        "tgkp,tgn->gkpn", scaled_grad, reading.reshape(row_count, group_count, N), precision=highest
    )
    _, end_grad = log_scan((own_decay, state_direct), SEQ, True, after_receive=during_backward)
    input_part, write_grad, read_grad, decay_grad, _ = ssd_pull((ssd_grad, end_grad))
    input_grad = skip_input_grad + input_part
    row_normed = lax.all_gather(tied["late_normed"], "sy", axis=0, tiled=True)
    row_partial = jnp.einsum(
        "txd,th->xdh", tied["columns"], row_normed, preferred_element_type=jnp.float32
    ).astype(jnp.bfloat16)
    weight_grad = lax.psum_scatter(row_partial, "sx", scatter_dimension=0, tiled=True).reshape(
        block, row_normed.shape[1]
    )
    return (
        layer_out,
        input_grad.astype(jnp.bfloat16),
        gate_grad.astype(jnp.bfloat16),
        write_grad.astype(jnp.bfloat16),
        read_grad.astype(jnp.bfloat16),
        decay_grad,
        weight_grad,
    )


def solution(mesh):
    in_specs = (
        P(SEQ, "head"),
        P(SEQ, "head"),
        P(SEQ, "head"),
        P(SEQ, "head"),
        P(SEQ, "head"),
        P("head"),
        P("head"),
        P(None, "head"),
        P(SEQ, "head"),
    )
    out_specs = (
        P(SEQ, "head"),
        P(SEQ, "head"),
        P(SEQ, "head"),
        P(SEQ, "head"),
        P(SEQ, "head"),
        P(SEQ, "head"),
        P(SEQ, "head"),
    )
    rows = mesh.devices.shape[0] // 4
    grid = Mesh(mesh.devices.reshape(rows, 4, mesh.devices.shape[1]), ("sx", "sy", "head"))
    return jax.shard_map(
        per_device, mesh=grid, in_specs=in_specs, out_specs=out_specs, check_vma=False
    )
```

```python
from functools import partial

import jax
import jax.numpy as jnp
from jax import lax
from jax.sharding import Mesh, PartitionSpec as P

HALF_HEADS = 128
P_SIZE = 64
N = 256
G = 8
SPAN = 256
SEQ = ("sx", "sy")


epsilon = 1e-05
highest = lax.Precision.HIGHEST


def shifted(x, axis, count, hop, reverse, cyclic):
    step = -hop if reverse else hop
    if cyclic:
        pairs = [(i, (i + step) % count) for i in range(count)]
    else:
        pairs = [(i, i + step) for i in range(count) if 0 <= i + step < count]
    return lax.ppermute(x, axis, pairs)


def earlier_part(place, got, count):
    decay = None
    state = None
    for hop in range(1, count):
        use = hop <= place
        got_decay, got_state = got[hop]
        if state is None:
            state = jnp.where(use, got_state, 0.0)
            decay = jnp.where(use, got_decay, 1.0)
        else:
            state = jnp.where(use, decay[..., None, None] * got_state + state, state)
            decay = jnp.where(use, decay * got_decay, decay)
    return decay, state


def two_level_scan(x, reverse):
    decay, state = x
    cols = lax.axis_size("sy")
    rows = lax.axis_size("sx")
    col = lax.axis_index("sy")
    row = lax.axis_index("sx")
    if reverse:
        col = cols - 1 - col
        row = rows - 1 - row
    sent = state.astype(jnp.bfloat16)
    got = {}
    for hop in range(1, cols):
        got[hop] = (
            shifted(decay, "sy", cols, hop, reverse, True),
            shifted(sent, "sy", cols, hop, reverse, True).astype(jnp.float32),
        )
    before_decay, before_state = earlier_part(col, got, cols)
    total_state = decay[..., None, None] * before_state + state
    total_decay = before_decay * decay
    for hop in range(cols - 1, 0, -1):
        use = hop >= col + 1
        got_decay, got_state = got[hop]
        total_state = jnp.where(use, got_decay[..., None, None] * total_state + got_state, total_state)
        total_decay = jnp.where(use, total_decay * got_decay, total_decay)
    sent_total = total_state.astype(jnp.bfloat16)
    got_rows = {}
    for hop in range(1, rows):
        got_rows[hop] = (
            shifted(total_decay, "sx", rows, hop, reverse, False),
            shifted(sent_total, "sx", rows, hop, reverse, False).astype(jnp.float32),
        )
    rows_decay, rows_state = earlier_part(row, got_rows, rows)
    return rows_decay * before_decay, before_decay[..., None, None] * rows_state + before_state


def block_scan(state_now, pieces):
    input_block, write_block, read_block, decay_block = pieces
    row_count = decay_block.shape[0]
    group_count, per_group = (state_now.shape[0], state_now.shape[1])
    input_heads = input_block.reshape(row_count, group_count, per_group, P_SIZE)
    write_heads = write_block.reshape(row_count, group_count, N)
    read_heads = read_block.reshape(row_count, group_count, N)
    cumulative = jnp.cumsum(decay_block, axis=0).reshape(row_count, group_count, per_group)
    by_head = jnp.transpose(cumulative, (1, 2, 0))
    causal = lax.broadcasted_iota(jnp.int32, (row_count, row_count), 0) >= lax.broadcasted_iota(
        jnp.int32, (row_count, row_count), 1
    )
    gap_table = jnp.where(causal, by_head[..., :, None] - by_head[..., None, :], 0.0)
    decay_table = jnp.where(causal, jnp.exp(gap_table), 0.0)
    scores = jnp.einsum("tgn,sgn->gts", read_heads, write_heads, precision=highest)
    weights = scores[:, None] * decay_table
    inner_sum = jnp.einsum("gkts,sgkp->tgkp", weights, input_heads, precision=highest)
    carried = jnp.einsum("tgn,gkpn->tgkp", read_heads, state_now, precision=highest)
    output = inner_sum + jnp.exp(cumulative)[..., None] * carried
    final_log = cumulative[-1]
    weighted = input_heads * jnp.exp(final_log[None] - cumulative)[..., None]
    fresh_state = jnp.einsum("sgkp,sgn->gkpn", weighted, write_heads, precision=highest)
    next_state = jnp.exp(final_log)[..., None, None] * state_now + fresh_state
    return (next_state, output.reshape(row_count, group_count * per_group * P_SIZE))


def block_end(state_now, pieces):
    input_block, write_block, decay_block = pieces
    row_count = decay_block.shape[0]
    group_count, per_group = (state_now.shape[0], state_now.shape[1])
    input_heads = input_block.reshape(row_count, group_count, per_group, P_SIZE)
    write_heads = write_block.reshape(row_count, group_count, N)
    cumulative = jnp.cumsum(decay_block, axis=0).reshape(row_count, group_count, per_group)
    final_log = cumulative[-1]
    weighted = input_heads * jnp.exp(final_log[None] - cumulative)[..., None]
    fresh_state = jnp.einsum("sgkp,sgn->gkpn", weighted, write_heads, precision=highest)
    return (jnp.exp(final_log)[..., None, None] * state_now + fresh_state, None)


def in_blocks(operand):
    return operand.reshape(operand.shape[0] // SPAN, SPAN, operand.shape[1])


def ssd_run(inputs, writes, reading, decays, start_state):
    row_count = decays.shape[0]
    final_state, outputs = lax.scan(
        block_scan,
        start_state,
        (in_blocks(inputs), in_blocks(writes), in_blocks(reading), in_blocks(decays)),
    )
    return (outputs.reshape(row_count, outputs.shape[2]), final_state)


def gate_norm(ssd_out, inputs, gate_values, skip_gain, norm_gain):
    row_count = ssd_out.shape[0]
    head_count = skip_gain.shape[0]
    direct = (inputs.reshape(row_count, head_count, P_SIZE) * skip_gain[:, None]).reshape(
        row_count, head_count * P_SIZE
    )
    gated_vals = (ssd_out + direct) * jax.nn.silu(gate_values)
    grouped = gated_vals.reshape(row_count, -1, HALF_HEADS * P_SIZE // G)
    factor = lax.rsqrt(jnp.mean(grouped * grouped, axis=2, keepdims=True) + epsilon)
    return (grouped * factor).reshape(row_count, head_count * P_SIZE) * norm_gain


def combine(earlier, later):
    return (earlier[0] * later[0], later[0][..., None, None] * earlier[1] + later[1])


def per_device(
    ssd_input,
    gate_input,
    write_vectors,
    read_vectors,
    log_decay,
    skip_gain,
    norm_gain,
    out_weight,
    out_grad,
):
    row_count, head_count = log_decay.shape
    group_count = write_vectors.shape[1] // N
    per_group = head_count // group_count
    inputs = ssd_input.astype(jnp.float32)
    gate_values = gate_input.astype(jnp.float32)
    writes = write_vectors.astype(jnp.float32)
    reading = read_vectors.astype(jnp.float32)
    zero_state = jnp.zeros((group_count, per_group, P_SIZE, N), jnp.float32)
    own_state, unused = lax.scan(
        block_end, zero_state, (in_blocks(inputs), in_blocks(writes), in_blocks(log_decay))
    )
    cumulative = jnp.cumsum(log_decay, axis=0)
    own_decay = jnp.exp(cumulative[-1]).reshape(group_count, per_group)
    decay_before, start_state = two_level_scan((own_decay, own_state), False)
    (ssd_out, end_state), ssd_pull = jax.vjp(
        ssd_run, inputs, writes, reading, log_decay, start_state
    )
    norm_fn = partial(gate_norm, skip_gain=skip_gain, norm_gain=norm_gain)
    normed, norm_pull = jax.vjp(norm_fn, ssd_out, inputs, gate_values)
    normed_half = normed.astype(jnp.bfloat16)
    partial_out = jnp.einsum(
        "th,dh->td", normed_half, out_weight, preferred_element_type=jnp.float32
    )
    layer_out = lax.psum_scatter(
        partial_out.astype(jnp.bfloat16), "head", scatter_dimension=1, tiled=True
    )
    full_grad = lax.all_gather(out_grad, "head", axis=1, tiled=True)
    normed_grad = jnp.dot(full_grad, out_weight, preferred_element_type=jnp.float32)
    ssd_grad, skip_input_grad, gate_grad = norm_pull(normed_grad)
    scaled_grad = ssd_grad.reshape(row_count, group_count, per_group, P_SIZE) * jnp.exp(
        cumulative
    ).reshape(row_count, group_count, per_group, 1)
    state_direct = jnp.einsum(
        "tgkp,tgn->gkpn", scaled_grad, reading.reshape(row_count, group_count, N), precision=highest
    )
    decay_after, end_grad = two_level_scan((own_decay, state_direct), True)
    input_part, write_grad, read_grad, decay_grad, start_grad = ssd_pull((ssd_grad, end_grad))
    input_grad = skip_input_grad + input_part
    rows = lax.axis_size("sx")
    cols = lax.axis_size("sy")
    feature_count = full_grad.shape[1]
    block = feature_count // (rows * cols)
    grad_columns = lax.all_to_all(
        full_grad.reshape(row_count, rows, cols, block),
        "sy",
        split_axis=2,
        concat_axis=0,
        tiled=True,
    ).reshape(cols * row_count, rows, block)
    row_normed = lax.all_gather(normed_half, "sy", axis=0, tiled=True)
    row_partial = jnp.einsum(
        "txd,th->xdh", grad_columns, row_normed, preferred_element_type=jnp.float32
    ).astype(jnp.bfloat16)
    weight_grad = lax.psum_scatter(row_partial, "sx", scatter_dimension=0, tiled=True).reshape(
        block, row_normed.shape[1]
    )
    return (
        layer_out,
        input_grad.astype(jnp.bfloat16),
        gate_grad.astype(jnp.bfloat16),
        write_grad.astype(jnp.bfloat16),
        read_grad.astype(jnp.bfloat16),
        decay_grad,
        weight_grad,
    )


def solution(mesh):
    in_specs = (
        P(SEQ, "head"),
        P(SEQ, "head"),
        P(SEQ, "head"),
        P(SEQ, "head"),
        P(SEQ, "head"),
        P("head"),
        P("head"),
        P(None, "head"),
        P(SEQ, "head"),
    )
    out_specs = (
        P(SEQ, "head"),
        P(SEQ, "head"),
        P(SEQ, "head"),
        P(SEQ, "head"),
        P(SEQ, "head"),
        P(SEQ, "head"),
        P(SEQ, "head"),
    )
    rows = mesh.devices.shape[0] // 4
    grid = Mesh(mesh.devices.reshape(rows, 4, mesh.devices.shape[1]), ("sx", "sy", "head"))
    return jax.shard_map(
        per_device, mesh=grid, in_specs=in_specs, out_specs=out_specs, check_vma=False
    )
```

```python
from functools import partial

import jax
import jax.numpy as jnp
from jax import lax
from jax.sharding import Mesh, PartitionSpec as P


HALF_HEADS = 128
P_SIZE = 64
N = 256
G = 8
SPAN = 256
SEQ = ("sx", "sy")


epsilon = 1e-05
highest = lax.Precision.HIGHEST


def shifted(x, axis, count, hop, reverse, cyclic):
    step = -hop if reverse else hop
    if cyclic:
        pairs = [(i, (i + step) % count) for i in range(count)]
    else:
        pairs = [(i, i + step) for i in range(count) if 0 <= i + step < count]
    return lax.ppermute(x, axis, pairs)


def earlier_part(place, got, count):
    decay = None
    state = None
    for hop in range(1, count):
        use = hop <= place
        got_decay, got_state = got[hop]
        if state is None:
            state = jnp.where(use, got_state, 0.0)
            decay = jnp.where(use, got_decay, 1.0)
        else:
            state = jnp.where(use, decay[..., None, None] * got_state + state, state)
            decay = jnp.where(use, decay * got_decay, decay)
    return decay, state


def two_level_scan(x, reverse):
    decay, state = x
    cols = lax.axis_size("sy")
    rows = lax.axis_size("sx")
    col = lax.axis_index("sy")
    row = lax.axis_index("sx")
    if reverse:
        col = cols - 1 - col
        row = rows - 1 - row
    sent = state.astype(jnp.bfloat16)
    got = {}
    for hop in range(1, cols):
        got[hop] = (
            shifted(decay, "sy", cols, hop, reverse, True),
            shifted(sent, "sy", cols, hop, reverse, True).astype(jnp.float32),
        )
    before_decay, before_state = earlier_part(col, got, cols)
    total_state = decay[..., None, None] * before_state + state
    total_decay = before_decay * decay
    for hop in range(cols - 1, 0, -1):
        use = hop >= col + 1
        got_decay, got_state = got[hop]
        total_state = jnp.where(use, got_decay[..., None, None] * total_state + got_state, total_state)
        total_decay = jnp.where(use, total_decay * got_decay, total_decay)
    sent_total = total_state.astype(jnp.bfloat16)
    got_rows = {}
    for hop in range(1, rows):
        got_rows[hop] = (
            shifted(total_decay, "sx", rows, hop, reverse, False),
            shifted(sent_total, "sx", rows, hop, reverse, False).astype(jnp.float32),
        )
    rows_decay, rows_state = earlier_part(row, got_rows, rows)
    return rows_decay * before_decay, before_decay[..., None, None] * rows_state + before_state


def block_scan(state_now, pieces):
    input_block, write_block, read_block, decay_block = pieces
    row_count = decay_block.shape[0]
    group_count, per_group = (state_now.shape[0], state_now.shape[1])
    input_heads = input_block.reshape(row_count, group_count, per_group, P_SIZE)
    write_heads = write_block.reshape(row_count, group_count, N)
    read_heads = read_block.reshape(row_count, group_count, N)
    cumulative = jnp.cumsum(decay_block, axis=0).reshape(row_count, group_count, per_group)
    by_head = jnp.transpose(cumulative, (1, 2, 0))
    causal = lax.broadcasted_iota(jnp.int32, (row_count, row_count), 0) >= lax.broadcasted_iota(
        jnp.int32, (row_count, row_count), 1
    )
    gap_table = jnp.where(causal, by_head[..., :, None] - by_head[..., None, :], 0.0)
    decay_table = jnp.where(causal, jnp.exp(gap_table), 0.0)
    scores = jnp.einsum("tgn,sgn->gts", read_heads, write_heads, precision=highest)
    weights = scores[:, None] * decay_table
    inner_sum = jnp.einsum("gkts,sgkp->tgkp", weights, input_heads, precision=highest)
    carried = jnp.einsum("tgn,gkpn->tgkp", read_heads, state_now, precision=highest)
    output = inner_sum + jnp.exp(cumulative)[..., None] * carried
    final_log = cumulative[-1]
    weighted = input_heads * jnp.exp(final_log[None] - cumulative)[..., None]
    fresh_state = jnp.einsum("sgkp,sgn->gkpn", weighted, write_heads, precision=highest)
    next_state = jnp.exp(final_log)[..., None, None] * state_now + fresh_state
    return (next_state, output.reshape(row_count, group_count * per_group * P_SIZE))


def block_end(state_now, pieces):
    input_block, write_block, decay_block = pieces
    row_count = decay_block.shape[0]
    group_count, per_group = (state_now.shape[0], state_now.shape[1])
    input_heads = input_block.reshape(row_count, group_count, per_group, P_SIZE)
    write_heads = write_block.reshape(row_count, group_count, N)
    cumulative = jnp.cumsum(decay_block, axis=0).reshape(row_count, group_count, per_group)
    final_log = cumulative[-1]
    weighted = input_heads * jnp.exp(final_log[None] - cumulative)[..., None]
    fresh_state = jnp.einsum("sgkp,sgn->gkpn", weighted, write_heads, precision=highest)
    return (jnp.exp(final_log)[..., None, None] * state_now + fresh_state, None)


def in_blocks(operand):
    return operand.reshape(operand.shape[0] // SPAN, SPAN, operand.shape[1])


def ssd_run(inputs, writes, reading, decays, start_state):
    row_count = decays.shape[0]
    final_state, outputs = lax.scan(
        block_scan,
        start_state,
        (in_blocks(inputs), in_blocks(writes), in_blocks(reading), in_blocks(decays)),
    )
    return (outputs.reshape(row_count, outputs.shape[2]), final_state)


def gate_norm(ssd_out, inputs, gate_values, skip_gain, norm_gain):
    row_count = ssd_out.shape[0]
    head_count = skip_gain.shape[0]
    direct = (inputs.reshape(row_count, head_count, P_SIZE) * skip_gain[:, None]).reshape(
        row_count, head_count * P_SIZE
    )
    gated_vals = (ssd_out + direct) * jax.nn.silu(gate_values)
    grouped = gated_vals.reshape(row_count, -1, HALF_HEADS * P_SIZE // G)
    factor = lax.rsqrt(jnp.mean(grouped * grouped, axis=2, keepdims=True) + epsilon)
    return (grouped * factor).reshape(row_count, head_count * P_SIZE) * norm_gain


def per_device(
    ssd_input,
    gate_input,
    write_vectors,
    read_vectors,
    log_decay,
    skip_gain,
    norm_gain,
    out_weight,
    out_grad,
):
    row_count, head_count = log_decay.shape
    group_count = write_vectors.shape[1] // N
    per_group = head_count // group_count
    inputs = ssd_input.astype(jnp.float32)
    gate_values = gate_input.astype(jnp.float32)
    writes = write_vectors.astype(jnp.float32)
    reading = read_vectors.astype(jnp.float32)
    zero_state = jnp.zeros((group_count, per_group, P_SIZE, N), jnp.float32)
    own_state, _ = lax.scan(
        block_end, zero_state, (in_blocks(inputs), in_blocks(writes), in_blocks(log_decay))
    )
    cumulative = jnp.cumsum(log_decay, axis=0)
    own_decay = jnp.exp(cumulative[-1]).reshape(group_count, per_group)
    _, start_state = two_level_scan((own_decay, own_state), False)
    (ssd_out, end_state), ssd_pull = jax.vjp(
        ssd_run, inputs, writes, reading, log_decay, start_state
    )
    norm_fn = partial(gate_norm, skip_gain=skip_gain, norm_gain=norm_gain)
    normed, norm_pull = jax.vjp(norm_fn, ssd_out, inputs, gate_values)
    normed_half = normed.astype(jnp.bfloat16)
    partial_out = jnp.einsum(
        "th,dh->td", normed_half, out_weight, preferred_element_type=jnp.float32
    )
    layer_out = lax.psum_scatter(
        partial_out.astype(jnp.bfloat16), "head", scatter_dimension=1, tiled=True
    )
    full_grad = lax.all_gather(out_grad, "head", axis=1, tiled=True)
    normed_grad = jnp.dot(full_grad, out_weight, preferred_element_type=jnp.float32)
    ssd_grad, skip_input_grad, gate_grad = norm_pull(normed_grad)
    scaled_grad = ssd_grad.reshape(row_count, group_count, per_group, P_SIZE) * jnp.exp(
        cumulative
    ).reshape(row_count, group_count, per_group, 1)
    state_direct = jnp.einsum(
        "tgkp,tgn->gkpn", scaled_grad, reading.reshape(row_count, group_count, N), precision=highest
    )
    _, end_grad = two_level_scan((own_decay, state_direct), True)
    input_part, write_grad, read_grad, decay_grad, _ = ssd_pull((ssd_grad, end_grad))
    input_grad = skip_input_grad + input_part
    rows = lax.axis_size("sx")
    cols = lax.axis_size("sy")
    feature_count = full_grad.shape[1]
    block = feature_count // (rows * cols)
    grad_columns = lax.all_to_all(
        full_grad.reshape(row_count, rows, cols, block),
        "sy",
        split_axis=2,
        concat_axis=0,
        tiled=True,
    ).reshape(cols * row_count, rows, block)
    row_normed = lax.all_gather(normed_half, "sy", axis=0, tiled=True)
    row_partial = jnp.einsum(
        "txd,th->xdh", grad_columns, row_normed, preferred_element_type=jnp.float32
    ).astype(jnp.bfloat16)
    weight_grad = lax.psum_scatter(row_partial, "sx", scatter_dimension=0, tiled=True).reshape(
        block, row_normed.shape[1]
    )
    return (
        layer_out,
        input_grad.astype(jnp.bfloat16),
        gate_grad.astype(jnp.bfloat16),
        write_grad.astype(jnp.bfloat16),
        read_grad.astype(jnp.bfloat16),
        decay_grad,
        weight_grad,
    )


def solution(mesh):
    in_specs = (
        P(SEQ, "head"),
        P(SEQ, "head"),
        P(SEQ, "head"),
        P(SEQ, "head"),
        P(SEQ, "head"),
        P("head"),
        P("head"),
        P(None, "head"),
        P(SEQ, "head"),
    )
    out_specs = (
        P(SEQ, "head"),
        P(SEQ, "head"),
        P(SEQ, "head"),
        P(SEQ, "head"),
        P(SEQ, "head"),
        P(SEQ, "head"),
        P(SEQ, "head"),
    )
    rows = mesh.devices.shape[0] // 4
    grid = Mesh(mesh.devices.reshape(rows, 4, mesh.devices.shape[1]), ("sx", "sy", "head"))
    return jax.shard_map(
        per_device, mesh=grid, in_specs=in_specs, out_specs=out_specs, check_vma=False
    )
```

```python
from functools import partial

import jax
import jax.numpy as jnp
from jax import lax
from jax.sharding import Mesh, PartitionSpec as P

HALF_HEADS = 128
P_SIZE = 64
N = 256
G = 8
SPAN = 256
SEQ = ("sx", "sy")


epsilon = 1e-05
highest = lax.Precision.HIGHEST


def shifted(x, axis, count, hop, reverse, cyclic):
    step = -hop if reverse else hop
    if cyclic:
        pairs = [(i, (i + step) % count) for i in range(count)]
    else:
        pairs = [(i, i + step) for i in range(count) if 0 <= i + step < count]
    return lax.ppermute(x, axis, pairs)


def earlier_part(place, got, count):
    decay = None
    state = None
    for hop in range(1, count):
        use = hop <= place
        got_decay, got_state = got[hop]
        if state is None:
            state = jnp.where(use, got_state, 0.0)
            decay = jnp.where(use, got_decay, 1.0)
        else:
            state = jnp.where(use, decay[..., None, None] * got_state + state, state)
            decay = jnp.where(use, decay * got_decay, decay)
    return decay, state


def two_level_scan(x, reverse, tie=None):
    decay, state = x
    cols = lax.axis_size("sy")
    rows = lax.axis_size("sx")
    col = lax.axis_index("sy")
    row = lax.axis_index("sx")
    if reverse:
        col = cols - 1 - col
        row = rows - 1 - row
    sent = state.astype(jnp.bfloat16)
    got = {}
    for hop in range(1, cols):
        got[hop] = (
            shifted(decay, "sy", cols, hop, reverse, True),
            shifted(sent, "sy", cols, hop, reverse, True).astype(jnp.float32),
        )
    before_decay, before_state = earlier_part(col, got, cols)
    total_state = decay[..., None, None] * before_state + state
    total_decay = before_decay * decay
    for hop in range(cols - 1, 0, -1):
        use = hop >= col + 1
        got_decay, got_state = got[hop]
        total_state = jnp.where(use, got_decay[..., None, None] * total_state + got_state, total_state)
        total_decay = jnp.where(use, total_decay * got_decay, total_decay)
    sent_total = total_state.astype(jnp.bfloat16)
    if tie is not None:
        sent_total, tie = lax.optimization_barrier((sent_total, tie))
    got_rows = {}
    for hop in range(1, rows):
        got_rows[hop] = (
            shifted(total_decay, "sx", rows, hop, reverse, False),
            shifted(sent_total, "sx", rows, hop, reverse, False).astype(jnp.float32),
        )
    rows_decay, rows_state = earlier_part(row, got_rows, rows)
    return (rows_decay * before_decay, before_decay[..., None, None] * rows_state + before_state), tie


def block_scan(state_now, pieces):
    input_block, write_block, read_block, decay_block = pieces
    row_count = decay_block.shape[0]
    group_count, per_group = (state_now.shape[0], state_now.shape[1])
    input_heads = input_block.reshape(row_count, group_count, per_group, P_SIZE)
    write_heads = write_block.reshape(row_count, group_count, N)
    read_heads = read_block.reshape(row_count, group_count, N)
    cumulative = jnp.cumsum(decay_block, axis=0).reshape(row_count, group_count, per_group)
    by_head = jnp.transpose(cumulative, (1, 2, 0))
    causal = lax.broadcasted_iota(jnp.int32, (row_count, row_count), 0) >= lax.broadcasted_iota(
        jnp.int32, (row_count, row_count), 1
    )
    gap_table = jnp.where(causal, by_head[..., :, None] - by_head[..., None, :], 0.0)
    decay_table = jnp.where(causal, jnp.exp(gap_table), 0.0)
    scores = jnp.einsum("tgn,sgn->gts", read_heads, write_heads, precision=highest)
    weights = scores[:, None] * decay_table
    inner_sum = jnp.einsum("gkts,sgkp->tgkp", weights, input_heads, precision=highest)
    carried = jnp.einsum("tgn,gkpn->tgkp", read_heads, state_now, precision=highest)
    output = inner_sum + jnp.exp(cumulative)[..., None] * carried
    final_log = cumulative[-1]
    weighted = input_heads * jnp.exp(final_log[None] - cumulative)[..., None]
    fresh_state = jnp.einsum("sgkp,sgn->gkpn", weighted, write_heads, precision=highest)
    next_state = jnp.exp(final_log)[..., None, None] * state_now + fresh_state
    return (next_state, output.reshape(row_count, group_count * per_group * P_SIZE))


def block_end(state_now, pieces):
    input_block, write_block, decay_block = pieces
    row_count = decay_block.shape[0]
    group_count, per_group = (state_now.shape[0], state_now.shape[1])
    input_heads = input_block.reshape(row_count, group_count, per_group, P_SIZE)
    write_heads = write_block.reshape(row_count, group_count, N)
    cumulative = jnp.cumsum(decay_block, axis=0).reshape(row_count, group_count, per_group)
    final_log = cumulative[-1]
    weighted = input_heads * jnp.exp(final_log[None] - cumulative)[..., None]
    fresh_state = jnp.einsum("sgkp,sgn->gkpn", weighted, write_heads, precision=highest)
    return (jnp.exp(final_log)[..., None, None] * state_now + fresh_state, None)


def in_blocks(operand):
    return operand.reshape(operand.shape[0] // SPAN, SPAN, operand.shape[1])


def ssd_run(inputs, writes, reading, decays, start_state):
    row_count = decays.shape[0]
    final_state, outputs = lax.scan(
        block_scan,
        start_state,
        (in_blocks(inputs), in_blocks(writes), in_blocks(reading), in_blocks(decays)),
    )
    return (outputs.reshape(row_count, outputs.shape[2]), final_state)


def gate_norm(ssd_out, inputs, gate_values, skip_gain, norm_gain):
    row_count = ssd_out.shape[0]
    head_count = skip_gain.shape[0]
    direct = (inputs.reshape(row_count, head_count, P_SIZE) * skip_gain[:, None]).reshape(
        row_count, head_count * P_SIZE
    )
    gated_vals = (ssd_out + direct) * jax.nn.silu(gate_values)
    grouped = gated_vals.reshape(row_count, -1, HALF_HEADS * P_SIZE // G)
    factor = lax.rsqrt(jnp.mean(grouped * grouped, axis=2, keepdims=True) + epsilon)
    return (grouped * factor).reshape(row_count, head_count * P_SIZE) * norm_gain


def combine(earlier, later):
    return (earlier[0] * later[0], later[0][..., None, None] * earlier[1] + later[1])


def per_device(
    ssd_input,
    gate_input,
    write_vectors,
    read_vectors,
    log_decay,
    skip_gain,
    norm_gain,
    out_weight,
    out_grad,
):
    row_count, head_count = log_decay.shape
    group_count = write_vectors.shape[1] // N
    per_group = head_count // group_count
    inputs = ssd_input.astype(jnp.float32)
    gate_values = gate_input.astype(jnp.float32)
    writes = write_vectors.astype(jnp.float32)
    reading = read_vectors.astype(jnp.float32)
    zero_state = jnp.zeros((group_count, per_group, P_SIZE, N), jnp.float32)
    own_state, unused = lax.scan(
        block_end, zero_state, (in_blocks(inputs), in_blocks(writes), in_blocks(log_decay))
    )
    cumulative = jnp.cumsum(log_decay, axis=0)
    own_decay = jnp.exp(cumulative[-1]).reshape(group_count, per_group)
    full_grad = lax.all_gather(out_grad, "head", axis=1, tiled=True)
    (decay_before, start_state), tied_grad = two_level_scan(
        (own_decay, own_state), False, full_grad
    )
    (ssd_out, end_state), ssd_pull = jax.vjp(
        ssd_run, inputs, writes, reading, log_decay, start_state
    )
    norm_fn = partial(gate_norm, skip_gain=skip_gain, norm_gain=norm_gain)
    normed, norm_pull = jax.vjp(norm_fn, ssd_out, inputs, gate_values)
    normed_half = normed.astype(jnp.bfloat16)
    partial_out = jnp.einsum(
        "th,dh->td", normed_half, out_weight, preferred_element_type=jnp.float32
    )
    layer_out = lax.psum_scatter(
        partial_out.astype(jnp.bfloat16), "head", scatter_dimension=1, tiled=True
    )
    normed_grad = jnp.dot(tied_grad, out_weight, preferred_element_type=jnp.float32)
    ssd_grad, skip_input_grad, gate_grad = norm_pull(normed_grad)
    scaled_grad = ssd_grad.reshape(row_count, group_count, per_group, P_SIZE) * jnp.exp(
        cumulative
    ).reshape(row_count, group_count, per_group, 1)
    state_direct = jnp.einsum(
        "tgkp,tgn->gkpn", scaled_grad, reading.reshape(row_count, group_count, N), precision=highest
    )
    (decay_after, end_grad), unused = two_level_scan((own_decay, state_direct), True)
    input_part, write_grad, read_grad, decay_grad, start_grad = ssd_pull((ssd_grad, end_grad))
    input_grad = skip_input_grad + input_part
    rows = lax.axis_size("sx")
    cols = lax.axis_size("sy")
    feature_count = full_grad.shape[1]
    block = feature_count // (rows * cols)
    grad_columns = lax.all_to_all(
        full_grad.reshape(row_count, rows, cols, block),
        "sy",
        split_axis=2,
        concat_axis=0,
        tiled=True,
    ).reshape(cols * row_count, rows, block)
    row_normed = lax.all_gather(normed_half, "sy", axis=0, tiled=True)
    row_partial = jnp.einsum(
        "txd,th->xdh", grad_columns, row_normed, preferred_element_type=jnp.float32
    ).astype(jnp.bfloat16)
    weight_grad = lax.psum_scatter(row_partial, "sx", scatter_dimension=0, tiled=True).reshape(
        block, row_normed.shape[1]
    )
    return (
        layer_out,
        input_grad.astype(jnp.bfloat16),
        gate_grad.astype(jnp.bfloat16),
        write_grad.astype(jnp.bfloat16),
        read_grad.astype(jnp.bfloat16),
        decay_grad,
        weight_grad,
    )


def solution(mesh):
    in_specs = (
        P(SEQ, "head"),
        P(SEQ, "head"),
        P(SEQ, "head"),
        P(SEQ, "head"),
        P(SEQ, "head"),
        P("head"),
        P("head"),
        P(None, "head"),
        P(SEQ, "head"),
    )
    out_specs = (
        P(SEQ, "head"),
        P(SEQ, "head"),
        P(SEQ, "head"),
        P(SEQ, "head"),
        P(SEQ, "head"),
        P(SEQ, "head"),
        P(SEQ, "head"),
    )
    rows = mesh.devices.shape[0] // 4
    grid = Mesh(mesh.devices.reshape(rows, 4, mesh.devices.shape[1]), ("sx", "sy", "head"))
    return jax.shard_map(
        per_device, mesh=grid, in_specs=in_specs, out_specs=out_specs, check_vma=False
    )
```

```python
from functools import partial

import jax
import jax.numpy as jnp
from jax import lax
from jax.sharding import Mesh, PartitionSpec as P


HALF_HEADS = 128
P_SIZE = 64
N = 256
G = 8
SPAN = 256
SEQ = ("sx", "sy")


epsilon = 1e-05
highest = lax.Precision.HIGHEST


def shifted(x, axis, count, hop, reverse, cyclic):
    step = -hop if reverse else hop
    if cyclic:
        pairs = [(i, (i + step) % count) for i in range(count)]
    else:
        pairs = [(i, i + step) for i in range(count) if 0 <= i + step < count]
    return lax.ppermute(x, axis, pairs)


def earlier_part(place, got, count):
    decay = None
    state = None
    for hop in range(1, count):
        use = hop <= place
        got_decay, got_state = got[hop]
        if state is None:
            state = jnp.where(use, got_state, 0.0)
            decay = jnp.where(use, got_decay, 1.0)
        else:
            state = jnp.where(use, decay[..., None, None] * got_state + state, state)
            decay = jnp.where(use, decay * got_decay, decay)
    return decay, state


def two_level_scan(x, reverse, tie=None):
    decay, state = x
    cols = lax.axis_size("sy")
    rows = lax.axis_size("sx")
    col = lax.axis_index("sy")
    row = lax.axis_index("sx")
    if reverse:
        col = cols - 1 - col
        row = rows - 1 - row
    sent = state.astype(jnp.bfloat16)
    got = {}
    for hop in range(1, cols):
        got[hop] = (
            shifted(decay, "sy", cols, hop, reverse, True),
            shifted(sent, "sy", cols, hop, reverse, True).astype(jnp.float32),
        )
    before_decay, before_state = earlier_part(col, got, cols)
    total_state = decay[..., None, None] * before_state + state
    total_decay = before_decay * decay
    for hop in range(cols - 1, 0, -1):
        use = hop >= col + 1
        got_decay, got_state = got[hop]
        total_state = jnp.where(use, got_decay[..., None, None] * total_state + got_state, total_state)
        total_decay = jnp.where(use, total_decay * got_decay, total_decay)
    sent_total = total_state.astype(jnp.bfloat16)
    if tie is not None:
        sent_total, tie = lax.optimization_barrier((sent_total, tie))
    got_rows = {}
    for hop in range(1, rows):
        got_rows[hop] = (
            shifted(total_decay, "sx", rows, hop, reverse, False),
            shifted(sent_total, "sx", rows, hop, reverse, False).astype(jnp.float32),
        )
    rows_decay, rows_state = earlier_part(row, got_rows, rows)
    return (rows_decay * before_decay, before_decay[..., None, None] * rows_state + before_state), tie


def block_scan(state_now, pieces):
    input_block, write_block, read_block, decay_block = pieces
    row_count = decay_block.shape[0]
    group_count, per_group = (state_now.shape[0], state_now.shape[1])
    input_heads = input_block.reshape(row_count, group_count, per_group, P_SIZE)
    write_heads = write_block.reshape(row_count, group_count, N)
    read_heads = read_block.reshape(row_count, group_count, N)
    cumulative = jnp.cumsum(decay_block, axis=0).reshape(row_count, group_count, per_group)
    by_head = jnp.transpose(cumulative, (1, 2, 0))
    causal = lax.broadcasted_iota(jnp.int32, (row_count, row_count), 0) >= lax.broadcasted_iota(
        jnp.int32, (row_count, row_count), 1
    )
    gap_table = jnp.where(causal, by_head[..., :, None] - by_head[..., None, :], 0.0)
    decay_table = jnp.where(causal, jnp.exp(gap_table), 0.0)
    scores = jnp.einsum("tgn,sgn->gts", read_heads, write_heads, precision=highest)
    weights = scores[:, None] * decay_table
    inner_sum = jnp.einsum("gkts,sgkp->tgkp", weights, input_heads, precision=highest)
    carried = jnp.einsum("tgn,gkpn->tgkp", read_heads, state_now, precision=highest)
    output = inner_sum + jnp.exp(cumulative)[..., None] * carried
    final_log = cumulative[-1]
    weighted = input_heads * jnp.exp(final_log[None] - cumulative)[..., None]
    fresh_state = jnp.einsum("sgkp,sgn->gkpn", weighted, write_heads, precision=highest)
    next_state = jnp.exp(final_log)[..., None, None] * state_now + fresh_state
    return (next_state, output.reshape(row_count, group_count * per_group * P_SIZE))


def block_end(state_now, pieces):
    input_block, write_block, decay_block = pieces
    row_count = decay_block.shape[0]
    group_count, per_group = (state_now.shape[0], state_now.shape[1])
    input_heads = input_block.reshape(row_count, group_count, per_group, P_SIZE)
    write_heads = write_block.reshape(row_count, group_count, N)
    cumulative = jnp.cumsum(decay_block, axis=0).reshape(row_count, group_count, per_group)
    final_log = cumulative[-1]
    weighted = input_heads * jnp.exp(final_log[None] - cumulative)[..., None]
    fresh_state = jnp.einsum("sgkp,sgn->gkpn", weighted, write_heads, precision=highest)
    return (jnp.exp(final_log)[..., None, None] * state_now + fresh_state, None)


def in_blocks(operand):
    return operand.reshape(operand.shape[0] // SPAN, SPAN, operand.shape[1])


def ssd_run(inputs, writes, reading, decays, start_state):
    row_count = decays.shape[0]
    final_state, outputs = lax.scan(
        block_scan,
        start_state,
        (in_blocks(inputs), in_blocks(writes), in_blocks(reading), in_blocks(decays)),
    )
    return (outputs.reshape(row_count, outputs.shape[2]), final_state)


def gate_norm(ssd_out, inputs, gate_values, skip_gain, norm_gain):
    row_count = ssd_out.shape[0]
    head_count = skip_gain.shape[0]
    direct = (inputs.reshape(row_count, head_count, P_SIZE) * skip_gain[:, None]).reshape(
        row_count, head_count * P_SIZE
    )
    gated_vals = (ssd_out + direct) * jax.nn.silu(gate_values)
    grouped = gated_vals.reshape(row_count, -1, HALF_HEADS * P_SIZE // G)
    factor = lax.rsqrt(jnp.mean(grouped * grouped, axis=2, keepdims=True) + epsilon)
    return (grouped * factor).reshape(row_count, head_count * P_SIZE) * norm_gain


def per_device(
    ssd_input,
    gate_input,
    write_vectors,
    read_vectors,
    log_decay,
    skip_gain,
    norm_gain,
    out_weight,
    out_grad,
):
    row_count, head_count = log_decay.shape
    group_count = write_vectors.shape[1] // N
    per_group = head_count // group_count
    inputs = ssd_input.astype(jnp.float32)
    gate_values = gate_input.astype(jnp.float32)
    writes = write_vectors.astype(jnp.float32)
    reading = read_vectors.astype(jnp.float32)
    zero_state = jnp.zeros((group_count, per_group, P_SIZE, N), jnp.float32)
    own_state, unused = lax.scan(
        block_end, zero_state, (in_blocks(inputs), in_blocks(writes), in_blocks(log_decay))
    )
    cumulative = jnp.cumsum(log_decay, axis=0)
    own_decay = jnp.exp(cumulative[-1]).reshape(group_count, per_group)
    full_grad = lax.all_gather(out_grad, "head", axis=1, tiled=True)
    (decay_before, start_state), tied_grad = two_level_scan(
        (own_decay, own_state), False, full_grad
    )
    (ssd_out, end_state), ssd_pull = jax.vjp(
        ssd_run, inputs, writes, reading, log_decay, start_state
    )
    norm_fn = partial(gate_norm, skip_gain=skip_gain, norm_gain=norm_gain)
    normed, norm_pull = jax.vjp(norm_fn, ssd_out, inputs, gate_values)
    normed_half = normed.astype(jnp.bfloat16)
    partial_out = jnp.einsum(
        "th,dh->td", normed_half, out_weight, preferred_element_type=jnp.float32
    )
    layer_out = lax.psum_scatter(
        partial_out.astype(jnp.bfloat16), "head", scatter_dimension=1, tiled=True
    )
    normed_grad = jnp.dot(tied_grad, out_weight, preferred_element_type=jnp.float32)
    ssd_grad, skip_input_grad, gate_grad = norm_pull(normed_grad)
    scaled_grad = ssd_grad.reshape(row_count, group_count, per_group, P_SIZE) * jnp.exp(
        cumulative
    ).reshape(row_count, group_count, per_group, 1)
    state_direct = jnp.einsum(
        "tgkp,tgn->gkpn", scaled_grad, reading.reshape(row_count, group_count, N), precision=highest
    )
    (decay_after, end_grad), unused = two_level_scan((own_decay, state_direct), True)
    input_part, write_grad, read_grad, decay_grad, _ = ssd_pull((ssd_grad, end_grad))
    input_grad = skip_input_grad + input_part
    rows = lax.axis_size("sx")
    cols = lax.axis_size("sy")
    feature_count = full_grad.shape[1]
    block = feature_count // (rows * cols)
    grad_columns = lax.all_to_all(
        full_grad.reshape(row_count, rows, cols, block),
        "sx",
        split_axis=1,
        concat_axis=0,
        tiled=True,
    ).reshape(rows * row_count, cols, block)
    column_normed = lax.all_gather(normed_half, "sx", axis=0, tiled=True)
    column_partial = jnp.einsum(
        "tyd,th->ydh", grad_columns, column_normed, preferred_element_type=jnp.float32
    ).astype(jnp.bfloat16)
    weight_grad = lax.psum_scatter(column_partial, "sy", scatter_dimension=0, tiled=True).reshape(
        block, column_normed.shape[1]
    )
    return (
        layer_out,
        input_grad.astype(jnp.bfloat16),
        gate_grad.astype(jnp.bfloat16),
        write_grad.astype(jnp.bfloat16),
        read_grad.astype(jnp.bfloat16),
        decay_grad,
        weight_grad,
    )


def solution(mesh):
    in_specs = (
        P(SEQ, "head"),
        P(SEQ, "head"),
        P(SEQ, "head"),
        P(SEQ, "head"),
        P(SEQ, "head"),
        P("head"),
        P("head"),
        P(None, "head"),
        P(SEQ, "head"),
    )
    out_specs = (
        P(SEQ, "head"),
        P(SEQ, "head"),
        P(SEQ, "head"),
        P(SEQ, "head"),
        P(SEQ, "head"),
        P(SEQ, "head"),
        P(SEQ, "head"),
    )
    rows = mesh.devices.shape[0] // 4
    grid = Mesh(mesh.devices.reshape(rows, 4, mesh.devices.shape[1]), ("sx", "sy", "head"))
    return jax.shard_map(
        per_device, mesh=grid, in_specs=in_specs, out_specs=out_specs, check_vma=False
    )
```

```python
from functools import partial

import jax
import jax.numpy as jnp
from jax import lax
from jax.sharding import Mesh, PartitionSpec as P


HALF_HEADS = 128
P_SIZE = 64
N = 256
G = 8
SPAN = 256
SEQ = ("sx", "sy")


epsilon = 1e-05
highest = lax.Precision.HIGHEST


def shifted(x, axis, count, hop, reverse, cyclic):
    step = -hop if reverse else hop
    if cyclic:
        pairs = [(i, (i + step) % count) for i in range(count)]
    else:
        pairs = [(i, i + step) for i in range(count) if 0 <= i + step < count]
    return lax.ppermute(x, axis, pairs)


def earlier_part(place, got, count):
    decay = None
    state = None
    for hop in range(1, count):
        use = hop <= place
        got_decay, got_state = got[hop]
        if state is None:
            state = jnp.where(use, got_state, 0.0)
            decay = jnp.where(use, got_decay, 1.0)
        else:
            state = jnp.where(use, decay[..., None, None] * got_state + state, state)
            decay = jnp.where(use, decay * got_decay, decay)
    return decay, state


def two_level_scan(x, reverse, tie=None, during=None):
    decay, state = x
    cols = lax.axis_size("sy")
    rows = lax.axis_size("sx")
    col = lax.axis_index("sy")
    row = lax.axis_index("sx")
    if reverse:
        col = cols - 1 - col
        row = rows - 1 - row
    sent = state.astype(jnp.bfloat16)
    got = {}
    for hop in range(1, cols):
        got[hop] = (
            shifted(decay, "sy", cols, hop, reverse, True),
            shifted(sent, "sy", cols, hop, reverse, True).astype(jnp.float32),
        )
    before_decay, before_state = earlier_part(col, got, cols)
    total_state = decay[..., None, None] * before_state + state
    total_decay = before_decay * decay
    for hop in range(cols - 1, 0, -1):
        use = hop >= col + 1
        got_decay, got_state = got[hop]
        total_state = jnp.where(use, got_decay[..., None, None] * total_state + got_state, total_state)
        total_decay = jnp.where(use, total_decay * got_decay, total_decay)
    sent_total = total_state.astype(jnp.bfloat16)
    if tie is not None:
        sent_total, tie = lax.optimization_barrier((sent_total, tie))
    got_rows = {}
    for hop in range(1, rows):
        got_rows[hop] = (
            shifted(total_decay, "sx", rows, hop, reverse, False),
            shifted(sent_total, "sx", rows, hop, reverse, False).astype(jnp.float32),
        )
    if during is not None:
        tie = during(tie)
        last = got_rows[rows - 1]
        last_state, tie = lax.optimization_barrier((last[1], tie))
        got_rows[rows - 1] = (last[0], last_state)
    rows_decay, rows_state = earlier_part(row, got_rows, rows)
    return (rows_decay * before_decay, before_decay[..., None, None] * rows_state + before_state), tie


def block_scan(state_now, pieces):
    input_block, write_block, read_block, decay_block = pieces
    row_count = decay_block.shape[0]
    group_count, per_group = (state_now.shape[0], state_now.shape[1])
    input_heads = input_block.reshape(row_count, group_count, per_group, P_SIZE)
    write_heads = write_block.reshape(row_count, group_count, N)
    read_heads = read_block.reshape(row_count, group_count, N)
    cumulative = jnp.cumsum(decay_block, axis=0).reshape(row_count, group_count, per_group)
    by_head = jnp.transpose(cumulative, (1, 2, 0))
    causal = lax.broadcasted_iota(jnp.int32, (row_count, row_count), 0) >= lax.broadcasted_iota(
        jnp.int32, (row_count, row_count), 1
    )
    gap_table = jnp.where(causal, by_head[..., :, None] - by_head[..., None, :], 0.0)
    decay_table = jnp.where(causal, jnp.exp(gap_table), 0.0)
    scores = jnp.einsum("tgn,sgn->gts", read_heads, write_heads, precision=highest)
    weights = scores[:, None] * decay_table
    inner_sum = jnp.einsum("gkts,sgkp->tgkp", weights, input_heads, precision=highest)
    carried = jnp.einsum("tgn,gkpn->tgkp", read_heads, state_now, precision=highest)
    output = inner_sum + jnp.exp(cumulative)[..., None] * carried
    final_log = cumulative[-1]
    weighted = input_heads * jnp.exp(final_log[None] - cumulative)[..., None]
    fresh_state = jnp.einsum("sgkp,sgn->gkpn", weighted, write_heads, precision=highest)
    next_state = jnp.exp(final_log)[..., None, None] * state_now + fresh_state
    return (next_state, output.reshape(row_count, group_count * per_group * P_SIZE))


def block_end(state_now, pieces):
    input_block, write_block, decay_block = pieces
    row_count = decay_block.shape[0]
    group_count, per_group = (state_now.shape[0], state_now.shape[1])
    input_heads = input_block.reshape(row_count, group_count, per_group, P_SIZE)
    write_heads = write_block.reshape(row_count, group_count, N)
    cumulative = jnp.cumsum(decay_block, axis=0).reshape(row_count, group_count, per_group)
    final_log = cumulative[-1]
    weighted = input_heads * jnp.exp(final_log[None] - cumulative)[..., None]
    fresh_state = jnp.einsum("sgkp,sgn->gkpn", weighted, write_heads, precision=highest)
    return (jnp.exp(final_log)[..., None, None] * state_now + fresh_state, None)


def in_blocks(operand):
    return operand.reshape(operand.shape[0] // SPAN, SPAN, operand.shape[1])


def ssd_run(inputs, writes, reading, decays, start_state):
    row_count = decays.shape[0]
    final_state, outputs = lax.scan(
        block_scan,
        start_state,
        (in_blocks(inputs), in_blocks(writes), in_blocks(reading), in_blocks(decays)),
    )
    return (outputs.reshape(row_count, outputs.shape[2]), final_state)


def gate_norm(ssd_out, inputs, gate_values, skip_gain, norm_gain):
    row_count = ssd_out.shape[0]
    head_count = skip_gain.shape[0]
    direct = (inputs.reshape(row_count, head_count, P_SIZE) * skip_gain[:, None]).reshape(
        row_count, head_count * P_SIZE
    )
    gated_vals = (ssd_out + direct) * jax.nn.silu(gate_values)
    grouped = gated_vals.reshape(row_count, -1, HALF_HEADS * P_SIZE // G)
    factor = lax.rsqrt(jnp.mean(grouped * grouped, axis=2, keepdims=True) + epsilon)
    return (grouped * factor).reshape(row_count, head_count * P_SIZE) * norm_gain


def per_device(
    ssd_input,
    gate_input,
    write_vectors,
    read_vectors,
    log_decay,
    skip_gain,
    norm_gain,
    out_weight,
    out_grad,
):
    row_count, head_count = log_decay.shape
    group_count = write_vectors.shape[1] // N
    per_group = head_count // group_count
    inputs = ssd_input.astype(jnp.float32)
    gate_values = gate_input.astype(jnp.float32)
    writes = write_vectors.astype(jnp.float32)
    reading = read_vectors.astype(jnp.float32)
    zero_state = jnp.zeros((group_count, per_group, P_SIZE, N), jnp.float32)
    own_state, unused = lax.scan(
        block_end, zero_state, (in_blocks(inputs), in_blocks(writes), in_blocks(log_decay))
    )
    cumulative = jnp.cumsum(log_decay, axis=0)
    own_decay = jnp.exp(cumulative[-1]).reshape(group_count, per_group)
    full_grad = lax.all_gather(out_grad, "head", axis=1, tiled=True)
    (decay_before, start_state), normed_grad = two_level_scan(
        (own_decay, own_state),
        False,
        full_grad,
        lambda grad: jnp.dot(grad, out_weight, preferred_element_type=jnp.float32),
    )
    (ssd_out, end_state), ssd_pull = jax.vjp(
        ssd_run, inputs, writes, reading, log_decay, start_state
    )
    norm_fn = partial(gate_norm, skip_gain=skip_gain, norm_gain=norm_gain)
    normed, norm_pull = jax.vjp(norm_fn, ssd_out, inputs, gate_values)
    normed_half = normed.astype(jnp.bfloat16)
    partial_out = jnp.einsum(
        "th,dh->td", normed_half, out_weight, preferred_element_type=jnp.float32
    )
    layer_out = lax.psum_scatter(
        partial_out.astype(jnp.bfloat16), "head", scatter_dimension=1, tiled=True
    )
    ssd_grad, skip_input_grad, gate_grad = norm_pull(normed_grad)
    scaled_grad = ssd_grad.reshape(row_count, group_count, per_group, P_SIZE) * jnp.exp(
        cumulative
    ).reshape(row_count, group_count, per_group, 1)
    state_direct = jnp.einsum(
        "tgkp,tgn->gkpn", scaled_grad, reading.reshape(row_count, group_count, N), precision=highest
    )
    (decay_after, end_grad), unused = two_level_scan((own_decay, state_direct), True)
    input_part, write_grad, read_grad, decay_grad, _ = ssd_pull((ssd_grad, end_grad))
    input_grad = skip_input_grad + input_part
    rows = lax.axis_size("sx")
    cols = lax.axis_size("sy")
    feature_count = full_grad.shape[1]
    block = feature_count // (rows * cols)
    grad_columns = lax.all_to_all(
        full_grad.reshape(row_count, rows, cols, block),
        "sx",
        split_axis=1,
        concat_axis=0,
        tiled=True,
    ).reshape(rows * row_count, cols, block)
    column_normed = lax.all_gather(normed_half, "sx", axis=0, tiled=True)
    column_partial = jnp.einsum(
        "tyd,th->ydh", grad_columns, column_normed, preferred_element_type=jnp.float32
    ).astype(jnp.bfloat16)
    weight_grad = lax.psum_scatter(
        column_partial, "sy", scatter_dimension=0, tiled=True
    ).reshape(block, column_normed.shape[1])
    return (
        layer_out,
        input_grad.astype(jnp.bfloat16),
        gate_grad.astype(jnp.bfloat16),
        write_grad.astype(jnp.bfloat16),
        read_grad.astype(jnp.bfloat16),
        decay_grad,
        weight_grad,
    )


def solution(mesh):
    in_specs = (
        P(SEQ, "head"),
        P(SEQ, "head"),
        P(SEQ, "head"),
        P(SEQ, "head"),
        P(SEQ, "head"),
        P("head"),
        P("head"),
        P(None, "head"),
        P(SEQ, "head"),
    )
    out_specs = (
        P(SEQ, "head"),
        P(SEQ, "head"),
        P(SEQ, "head"),
        P(SEQ, "head"),
        P(SEQ, "head"),
        P(SEQ, "head"),
        P(SEQ, "head"),
    )
    rows = mesh.devices.shape[0] // 4
    grid = Mesh(mesh.devices.reshape(rows, 4, mesh.devices.shape[1]), ("sx", "sy", "head"))
    return jax.shard_map(
        per_device, mesh=grid, in_specs=in_specs, out_specs=out_specs, check_vma=False
    )
```

```python
from functools import partial

import jax
import jax.numpy as jnp
from jax import lax
from jax.sharding import Mesh, PartitionSpec as P


HALF_HEADS = 128
P_SIZE = 64
N = 256
G = 8
SPAN = 256
SEQ = ("sx", "sy")


epsilon = 1e-05
highest = lax.Precision.HIGHEST


def shifted(x, axis, count, hop, reverse, cyclic):
    step = -hop if reverse else hop
    if cyclic:
        pairs = [(i, (i + step) % count) for i in range(count)]
    else:
        pairs = [(i, i + step) for i in range(count) if 0 <= i + step < count]
    return lax.ppermute(x, axis, pairs)


def earlier_part(place, got, count):
    decay = None
    state = None
    for hop in range(1, count):
        use = hop <= place
        got_decay, got_state = got[hop]
        if state is None:
            state = jnp.where(use, got_state, 0.0)
            decay = jnp.where(use, got_decay, 1.0)
        else:
            state = jnp.where(use, decay[..., None, None] * got_state + state, state)
            decay = jnp.where(use, decay * got_decay, decay)
    return decay, state


def two_level_scan(x, reverse, tie=None, during=None):
    decay, state = x
    cols = lax.axis_size("sy")
    rows = lax.axis_size("sx")
    col = lax.axis_index("sy")
    row = lax.axis_index("sx")
    if reverse:
        col = cols - 1 - col
        row = rows - 1 - row
    sent = state.astype(jnp.bfloat16)
    got = {}
    for hop in range(1, cols):
        got[hop] = (
            shifted(decay, "sy", cols, hop, reverse, True),
            shifted(sent, "sy", cols, hop, reverse, True).astype(jnp.float32),
        )
    before_decay, before_state = earlier_part(col, got, cols)
    total_state = decay[..., None, None] * before_state + state
    total_decay = before_decay * decay
    for hop in range(cols - 1, 0, -1):
        use = hop >= col + 1
        got_decay, got_state = got[hop]
        total_state = jnp.where(use, got_decay[..., None, None] * total_state + got_state, total_state)
        total_decay = jnp.where(use, total_decay * got_decay, total_decay)
    sent_total = total_state.astype(jnp.bfloat16)
    if tie is not None:
        sent_total, tie = lax.optimization_barrier((sent_total, tie))
    got_rows = {}
    for hop in range(1, rows):
        got_rows[hop] = (
            shifted(total_decay, "sx", rows, hop, reverse, False),
            shifted(sent_total, "sx", rows, hop, reverse, False).astype(jnp.float32),
        )
    if during is not None:
        tie = during(tie)
        last = got_rows[rows - 1]
        last_state, tie = lax.optimization_barrier((last[1], tie))
        got_rows[rows - 1] = (last[0], last_state)
    rows_decay, rows_state = earlier_part(row, got_rows, rows)
    return (rows_decay * before_decay, before_decay[..., None, None] * rows_state + before_state), tie


def block_scan(state_now, pieces):
    input_block, write_block, read_block, decay_block = pieces
    row_count = decay_block.shape[0]
    group_count, per_group = (state_now.shape[0], state_now.shape[1])
    input_heads = input_block.reshape(row_count, group_count, per_group, P_SIZE)
    write_heads = write_block.reshape(row_count, group_count, N)
    read_heads = read_block.reshape(row_count, group_count, N)
    cumulative = jnp.cumsum(decay_block, axis=0).reshape(row_count, group_count, per_group)
    by_head = jnp.transpose(cumulative, (1, 2, 0))
    causal = lax.broadcasted_iota(jnp.int32, (row_count, row_count), 0) >= lax.broadcasted_iota(
        jnp.int32, (row_count, row_count), 1
    )
    gap_table = jnp.where(causal, by_head[..., :, None] - by_head[..., None, :], 0.0)
    decay_table = jnp.where(causal, jnp.exp(gap_table), 0.0)
    scores = jnp.einsum("tgn,sgn->gts", read_heads, write_heads, precision=highest)
    weights = scores[:, None] * decay_table
    inner_sum = jnp.einsum("gkts,sgkp->tgkp", weights, input_heads, precision=highest)
    carried = jnp.einsum("tgn,gkpn->tgkp", read_heads, state_now, precision=highest)
    output = inner_sum + jnp.exp(cumulative)[..., None] * carried
    final_log = cumulative[-1]
    weighted = input_heads * jnp.exp(final_log[None] - cumulative)[..., None]
    fresh_state = jnp.einsum("sgkp,sgn->gkpn", weighted, write_heads, precision=highest)
    next_state = jnp.exp(final_log)[..., None, None] * state_now + fresh_state
    return (next_state, output.reshape(row_count, group_count * per_group * P_SIZE))


def block_end(state_now, pieces):
    input_block, write_block, decay_block = pieces
    row_count = decay_block.shape[0]
    group_count, per_group = (state_now.shape[0], state_now.shape[1])
    input_heads = input_block.reshape(row_count, group_count, per_group, P_SIZE)
    write_heads = write_block.reshape(row_count, group_count, N)
    cumulative = jnp.cumsum(decay_block, axis=0).reshape(row_count, group_count, per_group)
    final_log = cumulative[-1]
    weighted = input_heads * jnp.exp(final_log[None] - cumulative)[..., None]
    fresh_state = jnp.einsum("sgkp,sgn->gkpn", weighted, write_heads, precision=highest)
    return (jnp.exp(final_log)[..., None, None] * state_now + fresh_state, None)


def in_blocks(operand):
    return operand.reshape(operand.shape[0] // SPAN, SPAN, operand.shape[1])


def ssd_run(inputs, writes, reading, decays, start_state):
    row_count = decays.shape[0]
    final_state, outputs = lax.scan(
        block_scan,
        start_state,
        (in_blocks(inputs), in_blocks(writes), in_blocks(reading), in_blocks(decays)),
    )
    return (outputs.reshape(row_count, outputs.shape[2]), final_state)


def gate_norm(ssd_out, inputs, gate_values, skip_gain, norm_gain):
    row_count = ssd_out.shape[0]
    head_count = skip_gain.shape[0]
    direct = (inputs.reshape(row_count, head_count, P_SIZE) * skip_gain[:, None]).reshape(
        row_count, head_count * P_SIZE
    )
    gated_vals = (ssd_out + direct) * jax.nn.silu(gate_values)
    grouped = gated_vals.reshape(row_count, -1, HALF_HEADS * P_SIZE // G)
    factor = lax.rsqrt(jnp.mean(grouped * grouped, axis=2, keepdims=True) + epsilon)
    return (grouped * factor).reshape(row_count, head_count * P_SIZE) * norm_gain


def per_device(
    ssd_input,
    gate_input,
    write_vectors,
    read_vectors,
    log_decay,
    skip_gain,
    norm_gain,
    out_weight,
    out_grad,
):
    row_count, head_count = log_decay.shape
    group_count = write_vectors.shape[1] // N
    per_group = head_count // group_count
    inputs = ssd_input.astype(jnp.float32)
    gate_values = gate_input.astype(jnp.float32)
    writes = write_vectors.astype(jnp.float32)
    reading = read_vectors.astype(jnp.float32)
    zero_state = jnp.zeros((group_count, per_group, P_SIZE, N), jnp.float32)
    own_state, unused = lax.scan(
        block_end, zero_state, (in_blocks(inputs), in_blocks(writes), in_blocks(log_decay))
    )
    cumulative = jnp.cumsum(log_decay, axis=0)
    own_decay = jnp.exp(cumulative[-1]).reshape(group_count, per_group)
    full_grad = lax.all_gather(out_grad, "head", axis=1, tiled=True)
    rows = lax.axis_size("sx")
    cols = lax.axis_size("sy")
    row = lax.axis_index("sx")
    block = full_grad.shape[1] // (rows * cols)

    def during_rows(grad):
        by_row = grad.reshape(row_count, rows, cols, block)
        pieces = tuple(
            lax.dynamic_index_in_dim(by_row, (row + hop) % rows, 1, False) for hop in range(rows)
        )
        return jnp.dot(grad, out_weight, preferred_element_type=jnp.float32), pieces

    (decay_before, start_state), (normed_grad, pieces) = two_level_scan(
        (own_decay, own_state), False, full_grad, during_rows
    )
    (ssd_out, end_state), ssd_pull = jax.vjp(
        ssd_run, inputs, writes, reading, log_decay, start_state
    )
    norm_fn = partial(gate_norm, skip_gain=skip_gain, norm_gain=norm_gain)
    normed, norm_pull = jax.vjp(norm_fn, ssd_out, inputs, gate_values)
    normed_half = normed.astype(jnp.bfloat16)
    partial_out = jnp.einsum(
        "th,dh->td", normed_half, out_weight, preferred_element_type=jnp.float32
    )
    layer_out = lax.psum_scatter(
        partial_out.astype(jnp.bfloat16), "head", scatter_dimension=1, tiled=True
    )
    ssd_grad, skip_input_grad, gate_grad = norm_pull(normed_grad)
    scaled_grad = ssd_grad.reshape(row_count, group_count, per_group, P_SIZE) * jnp.exp(
        cumulative
    ).reshape(row_count, group_count, per_group, 1)
    state_direct = jnp.einsum(
        "tgkp,tgn->gkpn", scaled_grad, reading.reshape(row_count, group_count, N), precision=highest
    )
    (decay_after, end_grad), unused = two_level_scan((own_decay, state_direct), True)
    input_part, write_grad, read_grad, decay_grad, _ = ssd_pull((ssd_grad, end_grad))
    input_grad = skip_input_grad + input_part
    column_normed = lax.all_gather(normed_half, "sx", axis=0, tiled=True)
    arrived = [pieces[0]] + [
        lax.ppermute(pieces[hop], "sx", [(i, (i + hop) % rows) for i in range(rows)])
        for hop in range(1, rows)
    ]
    column_partial = None
    for hop in range(rows):
        source = (row - hop) % rows
        normed_rows = lax.dynamic_slice_in_dim(column_normed, source * row_count, row_count, 0)
        term = jnp.einsum(
            "tyd,th->ydh", arrived[hop], normed_rows, preferred_element_type=jnp.float32
        )
        column_partial = term if column_partial is None else column_partial + term
    column_partial = column_partial.astype(jnp.bfloat16)
    weight_grad = lax.psum_scatter(
        column_partial, "sy", scatter_dimension=0, tiled=True
    ).reshape(block, column_normed.shape[1])
    return (
        layer_out,
        input_grad.astype(jnp.bfloat16),
        gate_grad.astype(jnp.bfloat16),
        write_grad.astype(jnp.bfloat16),
        read_grad.astype(jnp.bfloat16),
        decay_grad,
        weight_grad,
    )


def solution(mesh):
    in_specs = (
        P(SEQ, "head"),
        P(SEQ, "head"),
        P(SEQ, "head"),
        P(SEQ, "head"),
        P(SEQ, "head"),
        P("head"),
        P("head"),
        P(None, "head"),
        P(SEQ, "head"),
    )
    out_specs = (
        P(SEQ, "head"),
        P(SEQ, "head"),
        P(SEQ, "head"),
        P(SEQ, "head"),
        P(SEQ, "head"),
        P(SEQ, "head"),
        P(SEQ, "head"),
    )
    rows = mesh.devices.shape[0] // 4
    grid = Mesh(mesh.devices.reshape(rows, 4, mesh.devices.shape[1]), ("sx", "sy", "head"))
    return jax.shard_map(
        per_device, mesh=grid, in_specs=in_specs, out_specs=out_specs, check_vma=False
    )
```
